256 devices in a mesh: layer: 64 (over y, z, core), blk: 4 (over x).
Axes of the slice: x: 4, y: 4, z: 8, core: 2. Of those that a mesh axis runs over, the one named last changes fastest.
Arguments:
- mode_matrix: bfloat16 [128, 512, 512], P(None, 'layer', 'blk'), may hold values from -1 to 1, as said below
- decay_rate: bfloat16 [128, 512], P(None, 'layer'), may hold values from 0.0009994507 to 0.29882812
- facet_refl: bfloat16 [128, 512], P(None, 'layer'), may hold values from -0.796875 to 0.796875
Outputs:
- prefix: bfloat16 [64, 4, 512, 512], P('layer', None, 'blk')
The draws below stay inside these ranges and needn't reach their ends.
Inputs may be any that keep to these rules, and one draw needn't show every extreme that they name: `mode_matrix`: each layer's matrix has orthonormal columns up to the rounding to bfloat16.
All inputs are finite; a program needn't handle non-finite values.
Results may differ from the reference program's by a relative error of at most 0.0045.
The reference program's roundings to bfloat16 on the way count: a program that leaves them out, or rounds other values in their place, can miss the bound.
Values may be sent and summed in bfloat16 or wider, within the bound.
No kernel may reach another device: no remote copies, remote signals or barrier semaphores. Data moves between devices by JAX's collectives and lax.ppermute only.
A program may use at most 64 MiB of HBM per device.

```python
import math
import jax
import jax.numpy as jnp
from jax import lax

HARM = 512
LAY_DEV = 2
REFL = 4
GROUPS = 64
LAYERS = 128
LEVELS = 6


def draw_mode_matrix(key, part):
    layer_keys = jax.random.split(key, LAYERS)

    def make_one(one_key):
        jitter = jax.random.normal(one_key, (HARM, HARM), jnp.float32) * (0.22 / math.sqrt(HARM))
        current = jnp.eye(HARM, dtype=jnp.float32) + jitter
        for repeat in range(8):
            gram = jnp.dot(current.T, current, precision=lax.Precision.HIGHEST)
            current = 1.5 * current - 0.5 * jnp.dot(current, gram, precision=lax.Precision.HIGHEST)
        return current.astype(jnp.bfloat16)
    return lax.map(make_one, layer_keys)


def levels(rng, shape, shards, least, largest):
    gain = 1.0
    for dim, parts in shards:
        steps = jax.random.uniform(jax.random.fold_in(jax.random.fold_in(rng, 6), dim), (parts,), jnp.float32, least / len(shards), largest / len(shards))
        gain = gain * jnp.repeat(jnp.exp(steps), shape[dim] // parts).reshape((-1,) + (1,) * (len(shape) - 1 - dim))
    return gain


def setup_inputs(seed: int = 0) -> dict:
    seeds = jax.random.split(jax.random.key(seed), 4)
    return {
        "mode_matrix": draw_mode_matrix(jax.random.fold_in(seeds[3], 71), 0),
        "decay_rate": jnp.clip(jnp.exp(math.log(0.29882812) - 5.700418 * jax.random.uniform(seeds[1], (LAYERS, HARM), jnp.float32) ** levels(seeds[1], (LAYERS, HARM), ((1, 64),), -0.2, 0.2)), 0.0009994507, 0.29882812).astype(jnp.bfloat16),
        "facet_refl": jnp.clip(jax.random.uniform(seeds[2], (LAYERS, HARM), jnp.float32, -0.796875, 0.796875) * levels(seeds[2], (LAYERS, HARM), ((1, 64),), -0.4, 0.0), -0.796875, 0.796875).astype(jnp.bfloat16),
    }


def times_f32(left_op, right_op):
    return jnp.dot(left_op, right_op, preferred_element_type=jnp.float32)

def star_product(upper_s, lower_s):
    coupling_down = times_f32(lower_s[0], upper_s[3]).astype(jnp.bfloat16)
    coupling_up = times_f32(upper_s[3], lower_s[0]).astype(jnp.bfloat16)
    left_sum = upper_s[1]
    for repeat in range(REFL):
        left_sum = (upper_s[1] + times_f32(left_sum, coupling_down)).astype(jnp.bfloat16)
    right_sum = lower_s[2]
    for repeat in range(REFL):
        right_sum = (lower_s[2] + times_f32(right_sum, coupling_up)).astype(jnp.bfloat16)
    left_mid = times_f32(left_sum, lower_s[0]).astype(jnp.bfloat16)
    right_mid = times_f32(right_sum, upper_s[3]).astype(jnp.bfloat16)
    new_refl = (upper_s[0] + times_f32(left_mid, upper_s[2])).astype(jnp.bfloat16)
    new_back = times_f32(left_sum, lower_s[1]).astype(jnp.bfloat16)
    new_fore = times_f32(right_sum, upper_s[2]).astype(jnp.bfloat16)
    new_under = (lower_s[3] + times_f32(right_mid, lower_s[1])).astype(jnp.bfloat16)
    return jnp.stack([new_refl, new_back, new_fore, new_under])

def layer_blocks(inputs):
    modes_one, decay_one, refl_one = inputs
    refl_full = refl_one.astype(jnp.float32)
    transmit = jnp.sqrt(1.0 - refl_full * refl_full) * jnp.exp(-decay_one.astype(jnp.float32))
    modes_wide = modes_one.astype(jnp.float32)
    scaled_refl = (modes_wide * refl_full[None, :]).astype(jnp.bfloat16)
    scaled_tran = (modes_wide * transmit[None, :]).astype(jnp.bfloat16)
    reflection = times_f32(modes_one, scaled_refl.T).astype(jnp.bfloat16)
    transmission = times_f32(modes_one, scaled_tran.T).astype(jnp.bfloat16)
    return jnp.stack([reflection, transmission, transmission, -reflection])

def group_fold(stack_group):
    running = stack_group[0]
    for layer_pos in range(1, LAY_DEV):
        running = star_product(running, stack_group[layer_pos])
    return running

def pair_star(operands):
    return star_product(operands[0], operands[1])

def reference(mode_matrix, decay_rate, facet_refl):
    layer_s = lax.map(layer_blocks, (mode_matrix, decay_rate, facet_refl))
    grouped = layer_s.reshape(GROUPS, LAY_DEV, 4, HARM, HARM)
    prefix = lax.map(group_fold, grouped)
    group_ids = jnp.arange(GROUPS, dtype=jnp.int32)
    for section_level in range(LEVELS):
        distance = 2 ** section_level
        shifted = jnp.concatenate([jnp.zeros_like(prefix[:distance]), prefix[:-distance]], axis=0)
        combined = lax.map(pair_star, (shifted, prefix))
        keep_new = (group_ids >= distance)[:, None, None, None]
        prefix = jnp.where(keep_new, combined, prefix)
    return prefix
```

```python
import jax
import jax.numpy as jnp
from jax import lax
from jax.sharding import PartitionSpec as P

HARM = 512
REFL = 4


def passed_along(value, axis, steps):
    count = lax.axis_size(axis)
    first, last = (max(0, -steps), min(count, count - steps))
    return lax.ppermute(value, axis, [(source, source + steps) for source in range(first, last)])


def times_f32(left_op, right_op):
    return jnp.dot(left_op, right_op, preferred_element_type=jnp.float32)


def star_whole(upper_s, lower_s):
    coupling_down = times_f32(lower_s[0], upper_s[3]).astype(jnp.bfloat16)
    coupling_up = times_f32(upper_s[3], lower_s[0]).astype(jnp.bfloat16)
    left_sum = upper_s[1]
    for repeat in range(REFL):
        left_sum = (upper_s[1] + times_f32(left_sum, coupling_down)).astype(jnp.bfloat16)
    right_sum = lower_s[2]
    for repeat in range(REFL):
        right_sum = (lower_s[2] + times_f32(right_sum, coupling_up)).astype(jnp.bfloat16)
    left_mid = times_f32(left_sum, lower_s[0]).astype(jnp.bfloat16)
    right_mid = times_f32(right_sum, upper_s[3]).astype(jnp.bfloat16)
    new_refl = (upper_s[0] + times_f32(left_mid, upper_s[2])).astype(jnp.bfloat16)
    new_back = times_f32(left_sum, lower_s[1]).astype(jnp.bfloat16)
    new_fore = times_f32(right_sum, upper_s[2]).astype(jnp.bfloat16)
    new_under = (lower_s[3] + times_f32(right_mid, lower_s[1])).astype(jnp.bfloat16)
    return jnp.stack([new_refl, new_back, new_fore, new_under])


def on_device(mode_matrix, decay_rate, facet_refl):
    relayed_modes, relayed_decay, relayed_refl = (
        lax.all_to_all(mode_matrix, "layer", split_axis=0, concat_axis=1, tiled=True),
        lax.all_to_all(decay_rate, "layer", split_axis=0, concat_axis=1, tiled=True),
        lax.all_to_all(facet_refl, "layer", split_axis=0, concat_axis=1, tiled=True),
    )
    block_index = lax.axis_index("blk")
    row_count = HARM // lax.axis_size("blk")
    row_start = block_index * row_count
    refl_full = relayed_refl.astype(jnp.float32)
    transmit = jnp.sqrt(1.0 - refl_full * refl_full) * jnp.exp(-relayed_decay.astype(jnp.float32))
    modes_all = lax.all_gather(relayed_modes, "blk", axis=2, tiled=True)
    modes_wide = modes_all.astype(jnp.float32)
    scaled_refl = (modes_wide * refl_full[:, None, :]).astype(jnp.bfloat16)
    scaled_tran = (modes_wide * transmit[:, None, :]).astype(jnp.bfloat16)
    refl_blk = jnp.einsum(
        "lhm,lkm->lhk", modes_all, scaled_refl, preferred_element_type=jnp.float32
    ).astype(jnp.bfloat16)
    tran_blk = jnp.einsum(
        "lhm,lkm->lhk", modes_all, scaled_tran, preferred_element_type=jnp.float32
    ).astype(jnp.bfloat16)
    layer_s = jnp.stack([refl_blk, tran_blk, tran_blk, -refl_blk], axis=1)
    whole_now = layer_s[0]
    for layer_pos in range(1, layer_s.shape[0]):
        whole_now = star_whole(whole_now, layer_s[layer_pos])
    group_index = lax.axis_index("layer")
    level_count = lax.axis_size("layer").bit_length() - 1
    for section_level in range(level_count):
        distance = 1 << section_level
        upper_whole = passed_along(whole_now, "layer", distance)
        combined = star_whole(upper_whole, whole_now)
        whole_now = jnp.where(group_index >= distance, combined, whole_now)
    own_rows = lax.dynamic_slice_in_dim(whole_now, row_start, row_count, 1)
    return own_rows[None]


def solution(mesh):
    placed = (P(None, "layer", "blk"), P(None, "layer"), P(None, "layer"))
    return jax.shard_map(
        on_device,
        mesh=mesh,
        in_specs=placed,
        out_specs=P("layer", None, "blk", None),
        check_vma=False,
    )
```

```python
import jax
import jax.numpy as jnp
from jax import lax
from jax.sharding import PartitionSpec as P
from jax.experimental import pallas as pl
from jax.experimental.pallas import tpu as pltpu

HARM = 512
REFL = 4


def passed_along(value, axis, steps):
    count = lax.axis_size(axis)
    first, last = (max(0, -steps), min(count, count - steps))
    return lax.ppermute(value, axis, [(source, source + steps) for source in range(first, last)])


def times_f32(left_op, right_op):
    return jnp.dot(left_op, right_op, preferred_element_type=jnp.float32)


def star_whole(upper_s, lower_s):
    coupling_down = times_f32(lower_s[0], upper_s[3]).astype(jnp.bfloat16)
    coupling_up = times_f32(upper_s[3], lower_s[0]).astype(jnp.bfloat16)
    left_sum = upper_s[1]
    for repeat in range(REFL):
        left_sum = (upper_s[1] + times_f32(left_sum, coupling_down)).astype(jnp.bfloat16)
    right_sum = lower_s[2]
    for repeat in range(REFL):
        right_sum = (lower_s[2] + times_f32(right_sum, coupling_up)).astype(jnp.bfloat16)
    left_mid = times_f32(left_sum, lower_s[0]).astype(jnp.bfloat16)
    right_mid = times_f32(right_sum, upper_s[3]).astype(jnp.bfloat16)
    new_refl = (upper_s[0] + times_f32(left_mid, upper_s[2])).astype(jnp.bfloat16)
    new_back = times_f32(left_sum, lower_s[1]).astype(jnp.bfloat16)
    new_fore = times_f32(right_sum, upper_s[2]).astype(jnp.bfloat16)
    new_under = (lower_s[3] + times_f32(right_mid, lower_s[1])).astype(jnp.bfloat16)
    return [new_refl, new_back, new_fore, new_under]


def star_kernel(flag_ref, upper_ref, lower_ref, out_ref):
    @pl.when(flag_ref[0] == 0)
    def _keep():
        out_ref[...] = lower_ref[...]

    @pl.when(flag_ref[0] != 0)
    def _combine():
        upper_s = [upper_ref[i] for i in range(4)]
        lower_s = [lower_ref[i] for i in range(4)]
        new_s = star_whole(upper_s, lower_s)
        for i in range(4):
            out_ref[i] = new_s[i]


def star_call(active, upper_s, lower_s):
    flag = active.astype(jnp.int32).reshape(1)
    return pl.pallas_call(
        star_kernel,
        out_shape=jax.ShapeDtypeStruct(lower_s.shape, lower_s.dtype),
        in_specs=[
            pl.BlockSpec(memory_space=pltpu.SMEM),
            pl.BlockSpec(memory_space=pltpu.VMEM),
            pl.BlockSpec(memory_space=pltpu.VMEM),
        ],
        out_specs=pl.BlockSpec(memory_space=pltpu.VMEM),
    )(flag, upper_s, lower_s)


def on_device(mode_matrix, decay_rate, facet_refl):
    relayed_modes, relayed_decay, relayed_refl = (
        lax.all_to_all(mode_matrix, "layer", split_axis=0, concat_axis=1, tiled=True),
        lax.all_to_all(decay_rate, "layer", split_axis=0, concat_axis=1, tiled=True),
        lax.all_to_all(facet_refl, "layer", split_axis=0, concat_axis=1, tiled=True),
    )
    block_index = lax.axis_index("blk")
    row_count = HARM // lax.axis_size("blk")
    row_start = block_index * row_count
    refl_full = relayed_refl.astype(jnp.float32)
    transmit = jnp.sqrt(1.0 - refl_full * refl_full) * jnp.exp(-relayed_decay.astype(jnp.float32))
    modes_all = lax.all_gather(relayed_modes, "blk", axis=2, tiled=True)
    modes_wide = modes_all.astype(jnp.float32)
    scaled_refl = (modes_wide * refl_full[:, None, :]).astype(jnp.bfloat16)
    scaled_tran = (modes_wide * transmit[:, None, :]).astype(jnp.bfloat16)
    refl_blk = jnp.einsum(
        "lhm,lkm->lhk", modes_all, scaled_refl, preferred_element_type=jnp.float32
    ).astype(jnp.bfloat16)
    tran_blk = jnp.einsum(
        "lhm,lkm->lhk", modes_all, scaled_tran, preferred_element_type=jnp.float32
    ).astype(jnp.bfloat16)
    layer_s = jnp.stack([refl_blk, tran_blk, tran_blk, -refl_blk], axis=1)
    whole_now = layer_s[0]
    for layer_pos in range(1, layer_s.shape[0]):
        whole_now = star_call(jnp.array(True), whole_now, layer_s[layer_pos])
    group_index = lax.axis_index("layer")
    level_count = lax.axis_size("layer").bit_length() - 1
    for section_level in range(level_count):
        distance = 1 << section_level
        upper_whole = passed_along(whole_now, "layer", distance)
        whole_now = star_call(group_index >= distance, upper_whole, whole_now)
    own_rows = lax.dynamic_slice_in_dim(whole_now, row_start, row_count, 1)
    return own_rows[None]


def solution(mesh):
    placed = (P(None, "layer", "blk"), P(None, "layer"), P(None, "layer"))
    return jax.shard_map(
        on_device,
        mesh=mesh,
        in_specs=placed,
        out_specs=P("layer", None, "blk", None),
        check_vma=False,
    )
```

```python
import functools

import jax
import jax.numpy as jnp
from jax import lax
from jax.sharding import PartitionSpec as P
from jax.experimental import pallas as pl
from jax.experimental.pallas import tpu as pltpu

HARM = 512
REFL = 4


def passed_along(value, axis, steps):
    count = lax.axis_size(axis)
    first, last = (max(0, -steps), min(count, count - steps))
    return lax.ppermute(value, axis, [(source, source + steps) for source in range(first, last)])


def rotated(value, axis, steps):
    count = lax.axis_size(axis)
    return lax.ppermute(value, axis, [(source, (source + steps) % count) for source in range(count)])


def times_f32(left_op, right_op):
    return jnp.dot(left_op, right_op, preferred_element_type=jnp.float32)


def star_whole(upper_s, lower_s):
    coupling_down = times_f32(lower_s[0], upper_s[3]).astype(jnp.bfloat16)
    coupling_up = times_f32(upper_s[3], lower_s[0]).astype(jnp.bfloat16)
    left_sum = upper_s[1]
    for repeat in range(REFL):
        left_sum = (upper_s[1] + times_f32(left_sum, coupling_down)).astype(jnp.bfloat16)
    right_sum = lower_s[2]
    for repeat in range(REFL):
        right_sum = (lower_s[2] + times_f32(right_sum, coupling_up)).astype(jnp.bfloat16)
    left_mid = times_f32(left_sum, lower_s[0]).astype(jnp.bfloat16)
    right_mid = times_f32(right_sum, upper_s[3]).astype(jnp.bfloat16)
    new_refl = (upper_s[0] + times_f32(left_mid, upper_s[2])).astype(jnp.bfloat16)
    new_back = times_f32(left_sum, lower_s[1]).astype(jnp.bfloat16)
    new_fore = times_f32(right_sum, upper_s[2]).astype(jnp.bfloat16)
    new_under = (lower_s[3] + times_f32(right_mid, lower_s[1])).astype(jnp.bfloat16)
    return [new_refl, new_back, new_fore, new_under]


def star_kernel(ctl_ref, upper_ref, lower_ref, out_ref, rows_ref, *, piece_count):
    active = ctl_ref[0]
    own_piece = ctl_ref[1]
    row_count = rows_ref.shape[1]

    @pl.when(active == 0)
    def _keep():
        out_ref[...] = lower_ref[...]

    @pl.when(active != 0)
    def _combine():
        if piece_count:
            upper_s = [
                jnp.concatenate(
                    [
                        upper_ref[(own_piece - source + piece_count) % piece_count, block]
                        for source in range(piece_count)
                    ],
                    axis=0,
                )
                for block in range(4)
            ]
        else:
            upper_s = [upper_ref[block] for block in range(4)]
        lower_s = [lower_ref[block] for block in range(4)]
        new_s = star_whole(upper_s, lower_s)
        for block in range(4):
            out_ref[block] = new_s[block]

    row_start = pl.multiple_of(own_piece * row_count, row_count)
    for block in range(4):
        rows_ref[block] = out_ref[block, pl.ds(row_start, row_count), :]


def star_call(active, own_piece, piece_count, upper_s, lower_s):
    ctl = jnp.stack([active.astype(jnp.int32), own_piece.astype(jnp.int32)])
    row_count = lower_s.shape[1] // max(piece_count, 1) if piece_count else lower_s.shape[1] // 4
    return pl.pallas_call(
        functools.partial(star_kernel, piece_count=piece_count),
        out_shape=(
            jax.ShapeDtypeStruct(lower_s.shape, lower_s.dtype),
            jax.ShapeDtypeStruct((4, row_count, lower_s.shape[2]), lower_s.dtype),
        ),
        in_specs=[
            pl.BlockSpec(memory_space=pltpu.SMEM),
            pl.BlockSpec(memory_space=pltpu.VMEM),
            pl.BlockSpec(memory_space=pltpu.VMEM),
        ],
        out_specs=(
            pl.BlockSpec(memory_space=pltpu.VMEM),
            pl.BlockSpec(memory_space=pltpu.VMEM),
        ),
    )(ctl, upper_s, lower_s)


def on_device(mode_matrix, decay_rate, facet_refl):
    coefficients = jnp.stack([decay_rate, facet_refl], axis=-1)
    relayed_modes = lax.all_to_all(mode_matrix, "layer", split_axis=0, concat_axis=1, tiled=True)
    relayed_coeff = lax.all_to_all(coefficients, "layer", split_axis=0, concat_axis=1, tiled=True)
    relayed_decay = relayed_coeff[..., 0]
    relayed_refl = relayed_coeff[..., 1]
    block_index = lax.axis_index("blk")
    block_count = lax.axis_size("blk")
    refl_full = relayed_refl.astype(jnp.float32)
    transmit = jnp.sqrt(1.0 - refl_full * refl_full) * jnp.exp(-relayed_decay.astype(jnp.float32))
    modes_all = lax.all_gather(relayed_modes, "blk", axis=2, tiled=True)
    modes_wide = modes_all.astype(jnp.float32)
    scaled_refl = (modes_wide * refl_full[:, None, :]).astype(jnp.bfloat16)
    scaled_tran = (modes_wide * transmit[:, None, :]).astype(jnp.bfloat16)
    refl_blk = jnp.einsum(
        "lhm,lkm->lhk", modes_all, scaled_refl, preferred_element_type=jnp.float32
    ).astype(jnp.bfloat16)
    tran_blk = jnp.einsum(
        "lhm,lkm->lhk", modes_all, scaled_tran, preferred_element_type=jnp.float32
    ).astype(jnp.bfloat16)
    layer_s = jnp.stack([refl_blk, tran_blk, tran_blk, -refl_blk], axis=1)
    whole_now = layer_s[0]
    own_rows = None
    for layer_pos in range(1, layer_s.shape[0]):
        whole_now, own_rows = star_call(
            jnp.array(True), block_index, 0, whole_now, layer_s[layer_pos]
        )
    group_index = lax.axis_index("layer")
    level_count = lax.axis_size("layer").bit_length() - 1
    for section_level in range(level_count):
        distance = 1 << section_level
        upper_rows = passed_along(own_rows, "layer", distance)
        pieces = [upper_rows] + [
            rotated(upper_rows, "blk", shift) for shift in range(1, block_count)
        ]
        whole_now, own_rows = star_call(
            group_index >= distance, block_index, block_count, jnp.stack(pieces), whole_now
        )
    return own_rows[None]


def solution(mesh):
    placed = (P(None, "layer", "blk"), P(None, "layer"), P(None, "layer"))
    return jax.shard_map(
        on_device,
        mesh=mesh,
        in_specs=placed,
        out_specs=P("layer", None, "blk", None),
        check_vma=False,
    )
```

```python
import functools

import jax
import jax.numpy as jnp
from jax import lax
from jax.sharding import PartitionSpec as P
from jax.experimental import pallas as pl
from jax.experimental.pallas import tpu as pltpu

HARM = 512
REFL = 4


def passed_along(value, axis, steps):
    count = lax.axis_size(axis)
    first, last = (max(0, -steps), min(count, count - steps))
    return lax.ppermute(value, axis, [(source, source + steps) for source in range(first, last)])


def rotated(value, axis, steps):
    count = lax.axis_size(axis)
    return lax.ppermute(value, axis, [(source, (source + steps) % count) for source in range(count)])


def times_f32(left_op, right_op):
    return jnp.dot(left_op, right_op, preferred_element_type=jnp.float32)


def star_whole(upper_s, lower_s):
    coupling_down = times_f32(lower_s[0], upper_s[3]).astype(jnp.bfloat16)
    coupling_up = times_f32(upper_s[3], lower_s[0]).astype(jnp.bfloat16)
    left_sum = upper_s[1]
    for repeat in range(REFL):
        left_sum = (upper_s[1] + times_f32(left_sum, coupling_down)).astype(jnp.bfloat16)
    right_sum = lower_s[2]
    for repeat in range(REFL):
        right_sum = (lower_s[2] + times_f32(right_sum, coupling_up)).astype(jnp.bfloat16)
    left_mid = times_f32(left_sum, lower_s[0]).astype(jnp.bfloat16)
    right_mid = times_f32(right_sum, upper_s[3]).astype(jnp.bfloat16)
    new_refl = (upper_s[0] + times_f32(left_mid, upper_s[2])).astype(jnp.bfloat16)
    new_back = times_f32(left_sum, lower_s[1]).astype(jnp.bfloat16)
    new_fore = times_f32(right_sum, upper_s[2]).astype(jnp.bfloat16)
    new_under = (lower_s[3] + times_f32(right_mid, lower_s[1])).astype(jnp.bfloat16)
    return [new_refl, new_back, new_fore, new_under]


HALVES = ((3, 1), (2, 0))


def star_kernel(ctl_ref, *refs, piece_count):
    if piece_count:
        half_refs, lower_ref, out_ref, row_refs = refs[:2], refs[2], refs[3], refs[4:]
    else:
        upper_ref, lower_ref, out_ref, row_refs = refs[0], refs[1], refs[2], refs[3:]
    active = ctl_ref[0]
    own_piece = ctl_ref[1]
    row_count = row_refs[0].shape[1]

    @pl.when(active == 0)
    def _keep():
        out_ref[...] = lower_ref[...]

    @pl.when(active != 0)
    def _combine():
        upper_s = [None] * 4
        if piece_count:
            for half_ref, half in zip(half_refs, HALVES):
                for slot, block in enumerate(half):
                    upper_s[block] = jnp.concatenate(
                        [
                            half_ref[(own_piece - source + piece_count) % piece_count, slot]
                            for source in range(piece_count)
                        ],
                        axis=0,
                    )
        else:
            upper_s = [upper_ref[block] for block in range(4)]
        lower_s = [lower_ref[block] for block in range(4)]
        new_s = star_whole(upper_s, lower_s)
        for block in range(4):
            out_ref[block] = new_s[block]

    row_start = pl.multiple_of(own_piece * row_count, row_count)
    for row_ref, half in zip(row_refs, HALVES):
        for slot, block in enumerate(half):
            row_ref[slot] = out_ref[block, pl.ds(row_start, row_count), :]


def star_call(active, own_piece, row_count, upper_parts, lower_s):
    ctl = jnp.stack([active.astype(jnp.int32), own_piece.astype(jnp.int32)])
    piece_count = upper_parts[0].shape[0] if len(upper_parts) == 2 else 0
    row_shape = jax.ShapeDtypeStruct((2, row_count, lower_s.shape[2]), lower_s.dtype)
    vmem = pl.BlockSpec(memory_space=pltpu.VMEM)
    return pl.pallas_call(
        functools.partial(star_kernel, piece_count=piece_count),
        out_shape=(jax.ShapeDtypeStruct(lower_s.shape, lower_s.dtype), row_shape, row_shape),
        in_specs=[pl.BlockSpec(memory_space=pltpu.SMEM)] + [vmem] * (len(upper_parts) + 1),
        out_specs=(vmem, vmem, vmem),
    )(ctl, *upper_parts, lower_s)


def on_device(mode_matrix, decay_rate, facet_refl):
    coefficients = jnp.stack([decay_rate, facet_refl], axis=-1)
    relayed_modes = lax.all_to_all(mode_matrix, "layer", split_axis=0, concat_axis=1, tiled=True)
    relayed_coeff = lax.all_to_all(coefficients, "layer", split_axis=0, concat_axis=1, tiled=True)
    relayed_decay = relayed_coeff[..., 0]
    relayed_refl = relayed_coeff[..., 1]
    block_index = lax.axis_index("blk")
    block_count = lax.axis_size("blk")
    refl_full = relayed_refl.astype(jnp.float32)
    transmit = jnp.sqrt(1.0 - refl_full * refl_full) * jnp.exp(-relayed_decay.astype(jnp.float32))
    modes_all = lax.all_gather(relayed_modes, "blk", axis=2, tiled=True)
    modes_wide = modes_all.astype(jnp.float32)
    scaled_refl = (modes_wide * refl_full[:, None, :]).astype(jnp.bfloat16)
    scaled_tran = (modes_wide * transmit[:, None, :]).astype(jnp.bfloat16)
    refl_blk = jnp.einsum(
        "lhm,lkm->lhk", modes_all, scaled_refl, preferred_element_type=jnp.float32
    ).astype(jnp.bfloat16)
    tran_blk = jnp.einsum(
        "lhm,lkm->lhk", modes_all, scaled_tran, preferred_element_type=jnp.float32
    ).astype(jnp.bfloat16)
    layer_s = jnp.stack([refl_blk, tran_blk, tran_blk, -refl_blk], axis=1)
    whole_now = layer_s[0]
    row_count = HARM // block_count
    own_halves = None
    for layer_pos in range(1, layer_s.shape[0]):
        whole_now, *own_halves = star_call(
            jnp.array(True), block_index, row_count, [whole_now], layer_s[layer_pos]
        )
    group_index = lax.axis_index("layer")
    level_count = lax.axis_size("layer").bit_length() - 1
    for section_level in range(level_count):
        distance = 1 << section_level
        upper_halves = []
        waiting = list(own_halves)
        while waiting:
            upper_rows = passed_along(waiting.pop(0), "layer", distance)
            if waiting:
                upper_rows, *waiting = lax.optimization_barrier([upper_rows] + waiting)
            pieces = [upper_rows] + [
                rotated(upper_rows, "blk", shift) for shift in range(1, block_count)
            ]
            upper_halves.append(jnp.stack(pieces))
        whole_now, *own_halves = star_call(
            group_index >= distance, block_index, row_count, upper_halves, whole_now
        )
    own_rows = jnp.stack([own_halves[1][1], own_halves[0][1], own_halves[1][0], own_halves[0][0]])
    return own_rows[None]


def solution(mesh):
    placed = (P(None, "layer", "blk"), P(None, "layer"), P(None, "layer"))
    return jax.shard_map(
        on_device,
        mesh=mesh,
        in_specs=placed,
        out_specs=P("layer", None, "blk", None),
        check_vma=False,
    )
```

```python
import functools

import jax
import jax.numpy as jnp
from jax import lax
from jax.sharding import PartitionSpec as P
from jax.experimental import pallas as pl
from jax.experimental.pallas import tpu as pltpu

HARM = 512
REFL = 4


def passed_along(value, axis, steps):
    count = lax.axis_size(axis)
    first, last = (max(0, -steps), min(count, count - steps))
    return lax.ppermute(value, axis, [(source, source + steps) for source in range(first, last)])


def rotated(value, axis, steps):
    count = lax.axis_size(axis)
    return lax.ppermute(value, axis, [(source, (source + steps) % count) for source in range(count)])


def times_f32(left_op, right_op):
    return jnp.dot(left_op, right_op, preferred_element_type=jnp.float32)


def star_whole(upper_s, lower_s):
    coupling_down = times_f32(lower_s[0], upper_s[3]).astype(jnp.bfloat16)
    coupling_up = times_f32(upper_s[3], lower_s[0]).astype(jnp.bfloat16)
    left_sum = upper_s[1]
    for repeat in range(REFL):
        left_sum = (upper_s[1] + times_f32(left_sum, coupling_down)).astype(jnp.bfloat16)
    right_sum = lower_s[2]
    for repeat in range(REFL):
        right_sum = (lower_s[2] + times_f32(right_sum, coupling_up)).astype(jnp.bfloat16)
    left_mid = times_f32(left_sum, lower_s[0]).astype(jnp.bfloat16)
    right_mid = times_f32(right_sum, upper_s[3]).astype(jnp.bfloat16)
    new_refl = (upper_s[0] + times_f32(left_mid, upper_s[2])).astype(jnp.bfloat16)
    new_back = times_f32(left_sum, lower_s[1]).astype(jnp.bfloat16)
    new_fore = times_f32(right_sum, upper_s[2]).astype(jnp.bfloat16)
    new_under = (lower_s[3] + times_f32(right_mid, lower_s[1])).astype(jnp.bfloat16)
    return [new_refl, new_back, new_fore, new_under]


HALVES = ((3, 1), (2, 0))


def star_kernel(ctl_ref, *refs, piece_count):
    if piece_count:
        half_refs, lower_ref, out_ref, row_refs = refs[:2], refs[2], refs[3], refs[4:]
    else:
        upper_ref, lower_ref, out_ref, row_refs = refs[0], refs[1], refs[2], refs[3:]
    active = ctl_ref[0]
    own_piece = ctl_ref[1]
    row_count = row_refs[0].shape[1]

    @pl.when(active == 0)
    def _keep():
        out_ref[...] = lower_ref[...]

    @pl.when(active != 0)
    def _combine():
        upper_s = [None] * 4
        if piece_count:
            for half_ref, half in zip(half_refs, HALVES):
                for slot, block in enumerate(half):
                    upper_s[block] = jnp.concatenate(
                        [half_ref[source, slot] for source in range(piece_count)],
                        axis=0,
                    )
        else:
            upper_s = [upper_ref[block] for block in range(4)]
        lower_s = [lower_ref[block] for block in range(4)]
        new_s = star_whole(upper_s, lower_s)
        for block in range(4):
            out_ref[block] = new_s[block]

    row_start = pl.multiple_of(own_piece * row_count, row_count)
    for row_ref, half in zip(row_refs, HALVES):
        for slot, block in enumerate(half):
            row_ref[slot] = out_ref[block, pl.ds(row_start, row_count), :]


def star_call(active, own_piece, row_count, upper_parts, lower_s):
    ctl = jnp.stack([active.astype(jnp.int32), own_piece.astype(jnp.int32)])
    piece_count = upper_parts[0].shape[0] if len(upper_parts) == 2 else 0
    row_shape = jax.ShapeDtypeStruct((2, row_count, lower_s.shape[2]), lower_s.dtype)
    vmem = pl.BlockSpec(memory_space=pltpu.VMEM)
    return pl.pallas_call(
        functools.partial(star_kernel, piece_count=piece_count),
        out_shape=(jax.ShapeDtypeStruct(lower_s.shape, lower_s.dtype), row_shape, row_shape),
        in_specs=[pl.BlockSpec(memory_space=pltpu.SMEM)] + [vmem] * (len(upper_parts) + 1),
        out_specs=(vmem, vmem, vmem),
    )(ctl, *upper_parts, lower_s)


def on_device(mode_matrix, decay_rate, facet_refl):
    coefficients = jnp.stack([decay_rate, facet_refl], axis=-1)
    relayed_modes = lax.all_to_all(mode_matrix, "layer", split_axis=0, concat_axis=1, tiled=True)
    relayed_coeff = lax.all_to_all(coefficients, "layer", split_axis=0, concat_axis=1, tiled=True)
    relayed_decay = relayed_coeff[..., 0]
    relayed_refl = relayed_coeff[..., 1]
    block_index = lax.axis_index("blk")
    block_count = lax.axis_size("blk")
    refl_full = relayed_refl.astype(jnp.float32)
    transmit = jnp.sqrt(1.0 - refl_full * refl_full) * jnp.exp(-relayed_decay.astype(jnp.float32))
    modes_all = lax.all_gather(relayed_modes, "blk", axis=2, tiled=True)
    modes_wide = modes_all.astype(jnp.float32)
    scaled_refl = (modes_wide * refl_full[:, None, :]).astype(jnp.bfloat16)
    scaled_tran = (modes_wide * transmit[:, None, :]).astype(jnp.bfloat16)
    refl_blk = jnp.einsum(
        "lhm,lkm->lhk", modes_all, scaled_refl, preferred_element_type=jnp.float32
    ).astype(jnp.bfloat16)
    tran_blk = jnp.einsum(
        "lhm,lkm->lhk", modes_all, scaled_tran, preferred_element_type=jnp.float32
    ).astype(jnp.bfloat16)
    layer_s = jnp.stack([refl_blk, tran_blk, tran_blk, -refl_blk], axis=1)
    whole_now = layer_s[0]
    row_count = HARM // block_count
    own_halves = None
    for layer_pos in range(1, layer_s.shape[0]):
        whole_now, *own_halves = star_call(
            jnp.array(True), block_index, row_count, [whole_now], layer_s[layer_pos]
        )
    group_index = lax.axis_index("layer")
    level_count = lax.axis_size("layer").bit_length() - 1
    for section_level in range(level_count):
        distance = 1 << section_level
        upper_halves = []
        waiting = list(own_halves)
        while waiting:
            upper_rows = passed_along(waiting.pop(0), "layer", distance)
            if waiting:
                upper_rows, *waiting = lax.optimization_barrier([upper_rows] + waiting)
            upper_halves.append(lax.all_gather(upper_rows, "blk", axis=0, tiled=False))
        whole_now, *own_halves = star_call(
            group_index >= distance, block_index, row_count, upper_halves, whole_now
        )
    own_rows = jnp.stack([own_halves[1][1], own_halves[0][1], own_halves[1][0], own_halves[0][0]])
    return own_rows[None]


def solution(mesh):
    placed = (P(None, "layer", "blk"), P(None, "layer"), P(None, "layer"))
    return jax.shard_map(
        on_device,
        mesh=mesh,
        in_specs=placed,
        out_specs=P("layer", None, "blk", None),
        check_vma=False,
    )
```

```python
import functools

import jax
import jax.numpy as jnp
from jax import lax
from jax.sharding import PartitionSpec as P
from jax.experimental import pallas as pl
from jax.experimental.pallas import tpu as pltpu

HARM = 512
REFL = 4


def passed_along(value, axis, steps):
    count = lax.axis_size(axis)
    first, last = (max(0, -steps), min(count, count - steps))
    return lax.ppermute(value, axis, [(source, source + steps) for source in range(first, last)])


def rotated(value, axis, steps):
    count = lax.axis_size(axis)
    return lax.ppermute(value, axis, [(source, (source + steps) % count) for source in range(count)])


def times_f32(left_op, right_op):
    return jnp.dot(left_op, right_op, preferred_element_type=jnp.float32)


def star_whole(upper_s, lower_s):
    coupling_down = times_f32(lower_s[0], upper_s[3]).astype(jnp.bfloat16)
    coupling_up = times_f32(upper_s[3], lower_s[0]).astype(jnp.bfloat16)

    def round_trip(repeat, sums):
        left_sum, right_sum = sums
        left_sum = (upper_s[1] + times_f32(left_sum, coupling_down)).astype(jnp.bfloat16)
        right_sum = (lower_s[2] + times_f32(right_sum, coupling_up)).astype(jnp.bfloat16)
        return left_sum, right_sum

    left_sum, right_sum = lax.fori_loop(0, REFL, round_trip, (upper_s[1], lower_s[2]))
    left_mid = times_f32(left_sum, lower_s[0]).astype(jnp.bfloat16)
    right_mid = times_f32(right_sum, upper_s[3]).astype(jnp.bfloat16)
    new_refl = (upper_s[0] + times_f32(left_mid, upper_s[2])).astype(jnp.bfloat16)
    new_back = times_f32(left_sum, lower_s[1]).astype(jnp.bfloat16)
    new_fore = times_f32(right_sum, upper_s[2]).astype(jnp.bfloat16)
    new_under = (lower_s[3] + times_f32(right_mid, lower_s[1])).astype(jnp.bfloat16)
    return [new_refl, new_back, new_fore, new_under]


HALVES = ((3, 1), (2, 0))


def star_kernel(ctl_ref, *refs, piece_count):
    if piece_count:
        half_refs, lower_ref, out_ref, row_refs = refs[:2], refs[2], refs[3], refs[4:]
    else:
        upper_ref, lower_ref, out_ref, row_refs = refs[0], refs[1], refs[2], refs[3:]
    active = ctl_ref[0]
    own_piece = ctl_ref[1]
    row_count = row_refs[0].shape[1]

    @pl.when(active == 0)
    def _keep():
        out_ref[...] = lower_ref[...]

    @pl.when(active != 0)
    def _combine():
        upper_s = [None] * 4
        if piece_count:
            for half_ref, half in zip(half_refs, HALVES):
                for slot, block in enumerate(half):
                    upper_s[block] = jnp.concatenate(
                        [
                            half_ref[(own_piece - source + piece_count) % piece_count, slot]
                            for source in range(piece_count)
                        ],
                        axis=0,
                    )
        else:
            upper_s = [upper_ref[block] for block in range(4)]
        lower_s = [lower_ref[block] for block in range(4)]
        new_s = star_whole(upper_s, lower_s)
        for block in range(4):
            out_ref[block] = new_s[block]

    row_start = pl.multiple_of(own_piece * row_count, row_count)
    for row_ref, half in zip(row_refs, HALVES):
        for slot, block in enumerate(half):
            row_ref[slot] = out_ref[block, pl.ds(row_start, row_count), :]


def star_call(active, own_piece, row_count, upper_parts, lower_s):
    ctl = jnp.stack([active.astype(jnp.int32), own_piece.astype(jnp.int32)])
    piece_count = upper_parts[0].shape[0] if len(upper_parts) == 2 else 0
    row_shape = jax.ShapeDtypeStruct((2, row_count, lower_s.shape[2]), lower_s.dtype)
    vmem = pl.BlockSpec(memory_space=pltpu.VMEM)
    return pl.pallas_call(
        functools.partial(star_kernel, piece_count=piece_count),
        out_shape=(jax.ShapeDtypeStruct(lower_s.shape, lower_s.dtype), row_shape, row_shape),
        in_specs=[pl.BlockSpec(memory_space=pltpu.SMEM)] + [vmem] * (len(upper_parts) + 1),
        out_specs=(vmem, vmem, vmem),
    )(ctl, *upper_parts, lower_s)


def on_device(mode_matrix, decay_rate, facet_refl):
    group_count = lax.axis_size("layer")
    layer_total, harm_part, mode_part = mode_matrix.shape
    layers_here = layer_total // group_count
    coefficients = jnp.stack([decay_rate, facet_refl], axis=-1)
    packed = jnp.concatenate(
        [
            mode_matrix.reshape(layer_total, harm_part * mode_part),
            coefficients.reshape(layer_total, harm_part * 2),
        ],
        axis=1,
    ).reshape(group_count, layers_here, -1)
    relayed = lax.all_to_all(packed, "layer", split_axis=0, concat_axis=0, tiled=True)
    relayed_modes = (
        relayed[:, :, : harm_part * mode_part]
        .reshape(group_count, layers_here, harm_part, mode_part)
        .transpose(1, 0, 2, 3)
        .reshape(layers_here, group_count * harm_part, mode_part)
    )
    relayed_coeff = (
        relayed[:, :, harm_part * mode_part :]
        .reshape(group_count, layers_here, harm_part, 2)
        .transpose(1, 0, 2, 3)
        .reshape(layers_here, group_count * harm_part, 2)
    )
    relayed_decay = relayed_coeff[..., 0]
    relayed_refl = relayed_coeff[..., 1]
    block_index = lax.axis_index("blk")
    block_count = lax.axis_size("blk")
    refl_full = relayed_refl.astype(jnp.float32)
    transmit = jnp.sqrt(1.0 - refl_full * refl_full) * jnp.exp(-relayed_decay.astype(jnp.float32))
    modes_all = lax.all_gather(relayed_modes, "blk", axis=2, tiled=True)
    modes_wide = modes_all.astype(jnp.float32)
    scaled_refl = (modes_wide * refl_full[:, None, :]).astype(jnp.bfloat16)
    scaled_tran = (modes_wide * transmit[:, None, :]).astype(jnp.bfloat16)
    refl_blk = jnp.einsum(
        "lhm,lkm->lhk", modes_all, scaled_refl, preferred_element_type=jnp.float32
    ).astype(jnp.bfloat16)
    tran_blk = jnp.einsum(
        "lhm,lkm->lhk", modes_all, scaled_tran, preferred_element_type=jnp.float32
    ).astype(jnp.bfloat16)
    layer_s = jnp.stack([refl_blk, tran_blk, tran_blk, -refl_blk], axis=1)
    whole_now = layer_s[0]
    row_count = HARM // block_count
    own_halves = None
    for layer_pos in range(1, layer_s.shape[0]):
        whole_now, *own_halves = star_call(
            jnp.array(True), block_index, row_count, [whole_now], layer_s[layer_pos]
        )
    group_index = lax.axis_index("layer")
    level_count = lax.axis_size("layer").bit_length() - 1
    for section_level in range(level_count):
        distance = 1 << section_level
        upper_halves = []
        waiting = list(own_halves)
        while waiting:
            upper_rows = passed_along(waiting.pop(0), "layer", distance)
            if waiting:
                upper_rows, *waiting = lax.optimization_barrier([upper_rows] + waiting)
            pieces = [upper_rows] + [
                rotated(upper_rows, "blk", shift) for shift in range(1, block_count)
            ]
            upper_halves.append(jnp.stack(pieces))
        whole_now, *own_halves = star_call(
            group_index >= distance, block_index, row_count, upper_halves, whole_now
        )
    own_rows = jnp.stack([own_halves[1][1], own_halves[0][1], own_halves[1][0], own_halves[0][0]])
    return own_rows[None]


def solution(mesh):
    placed = (P(None, "layer", "blk"), P(None, "layer"), P(None, "layer"))
    return jax.shard_map(
        on_device,
        mesh=mesh,
        in_specs=placed,
        out_specs=P("layer", None, "blk", None),
        check_vma=False,
    )
```

```python
import functools

import jax
import jax.numpy as jnp
from jax import lax
from jax.sharding import PartitionSpec as P
from jax.experimental import pallas as pl
from jax.experimental.pallas import tpu as pltpu

HARM = 512
REFL = 4


def passed_along(value, axis, steps):
    count = lax.axis_size(axis)
    first, last = (max(0, -steps), min(count, count - steps))
    return lax.ppermute(value, axis, [(source, source + steps) for source in range(first, last)])


def rotated(value, axis, steps):
    count = lax.axis_size(axis)
    return lax.ppermute(value, axis, [(source, (source + steps) % count) for source in range(count)])


def times_f32(left_op, right_op):
    return jnp.dot(left_op, right_op, preferred_element_type=jnp.float32)


def star_whole(upper_s, lower_s):
    coupling_down = times_f32(lower_s[0], upper_s[3]).astype(jnp.bfloat16)
    coupling_up = times_f32(upper_s[3], lower_s[0]).astype(jnp.bfloat16)
    left_sum = upper_s[1]
    for repeat in range(REFL):
        left_sum = (upper_s[1] + times_f32(left_sum, coupling_down)).astype(jnp.bfloat16)
    right_sum = lower_s[2]
    for repeat in range(REFL):
        right_sum = (lower_s[2] + times_f32(right_sum, coupling_up)).astype(jnp.bfloat16)
    left_mid = times_f32(left_sum, lower_s[0]).astype(jnp.bfloat16)
    right_mid = times_f32(right_sum, upper_s[3]).astype(jnp.bfloat16)
    new_refl = (upper_s[0] + times_f32(left_mid, upper_s[2])).astype(jnp.bfloat16)
    new_back = times_f32(left_sum, lower_s[1]).astype(jnp.bfloat16)
    new_fore = times_f32(right_sum, upper_s[2]).astype(jnp.bfloat16)
    new_under = (lower_s[3] + times_f32(right_mid, lower_s[1])).astype(jnp.bfloat16)
    return [new_refl, new_back, new_fore, new_under]


def assembled(pieces_ref, slot, own_piece):
    piece_count = pieces_ref.shape[0]
    return jnp.concatenate(
        [
            pieces_ref[(own_piece - source + piece_count) % piece_count, slot]
            for source in range(piece_count)
        ],
        axis=0,
    )


def first_kernel(ctl_ref, upper_ref, lower_ref, top_ref, bottom_ref, whole_ref):
    own_piece = ctl_ref[0]
    row_count = top_ref.shape[1]
    new_s = star_whole(
        [upper_ref[block] for block in range(4)], [lower_ref[block] for block in range(4)]
    )
    for block in range(4):
        whole_ref[block] = new_s[block]
    row_start = pl.multiple_of(own_piece * row_count, row_count)
    for slot, block in enumerate((3, 2)):
        top_ref[slot] = whole_ref[block, pl.ds(row_start, row_count), :]
    for slot, block in enumerate((1, 0)):
        bottom_ref[slot] = whole_ref[block, pl.ds(row_start, row_count), :]


def level_kernel(
    ctl_ref, far_ref, near_ref, lower_far_ref, top_ref, bottom_ref, new_top_ref, new_bottom_ref
):
    active = ctl_ref[0]
    own_piece = ctl_ref[1]

    @pl.when(active == 0)
    def _keep():
        new_top_ref[...] = top_ref[...]
        new_bottom_ref[...] = bottom_ref[...]

    @pl.when(active != 0)
    def _combine():
        a22 = assembled(far_ref, 0, own_piece)
        a21 = assembled(far_ref, 1, own_piece)
        a12 = near_ref[0]
        a11 = near_ref[1]
        b12 = assembled(lower_far_ref, 0, own_piece)
        b11 = assembled(lower_far_ref, 1, own_piece)
        b22 = top_ref[0]
        b21 = top_ref[1]
        coupling_down = times_f32(b11, a22).astype(jnp.bfloat16)
        coupling_up = times_f32(a22, b11).astype(jnp.bfloat16)
        left_sum = a12
        for repeat in range(REFL):
            left_sum = (a12 + times_f32(left_sum, coupling_down)).astype(jnp.bfloat16)
        right_sum = b21
        for repeat in range(REFL):
            right_sum = (b21 + times_f32(right_sum, coupling_up)).astype(jnp.bfloat16)
        left_mid = times_f32(left_sum, b11).astype(jnp.bfloat16)
        right_mid = times_f32(right_sum, a22).astype(jnp.bfloat16)
        new_bottom_ref[1] = (a11 + times_f32(left_mid, a21)).astype(jnp.bfloat16)
        new_bottom_ref[0] = times_f32(left_sum, b12).astype(jnp.bfloat16)
        new_top_ref[1] = times_f32(right_sum, a21).astype(jnp.bfloat16)
        new_top_ref[0] = (b22 + times_f32(right_mid, b12)).astype(jnp.bfloat16)


def first_call(own_piece, row_count, upper_s, lower_s):
    ctl = own_piece.astype(jnp.int32).reshape(1)
    row_shape = jax.ShapeDtypeStruct((2, row_count, lower_s.shape[2]), lower_s.dtype)
    vmem = pl.BlockSpec(memory_space=pltpu.VMEM)
    return pl.pallas_call(
        first_kernel,
        out_shape=(row_shape, row_shape),
        in_specs=[pl.BlockSpec(memory_space=pltpu.SMEM), vmem, vmem],
        out_specs=(vmem, vmem),
        scratch_shapes=[pltpu.VMEM(lower_s.shape, lower_s.dtype)],
    )(ctl, upper_s, lower_s)


def level_call(active, own_piece, far, near, lower_far, top, bottom):
    ctl = jnp.stack([active.astype(jnp.int32), own_piece.astype(jnp.int32)])
    row_shape = jax.ShapeDtypeStruct(top.shape, top.dtype)
    vmem = pl.BlockSpec(memory_space=pltpu.VMEM)
    return pl.pallas_call(
        level_kernel,
        out_shape=(row_shape, row_shape),
        in_specs=[pl.BlockSpec(memory_space=pltpu.SMEM)] + [vmem] * 5,
        out_specs=(vmem, vmem),
    )(ctl, far, near, lower_far, top, bottom)


def spread(value, axis):
    count = lax.axis_size(axis)
    return jnp.stack([value] + [rotated(value, axis, shift) for shift in range(1, count)])


def on_device(mode_matrix, decay_rate, facet_refl):
    coefficients = jnp.stack([decay_rate, facet_refl], axis=-1)
    relayed_modes = lax.all_to_all(mode_matrix, "layer", split_axis=0, concat_axis=1, tiled=True)
    relayed_coeff = lax.all_to_all(coefficients, "layer", split_axis=0, concat_axis=1, tiled=True)
    relayed_decay = relayed_coeff[..., 0]
    relayed_refl = relayed_coeff[..., 1]
    block_index = lax.axis_index("blk")
    block_count = lax.axis_size("blk")
    refl_full = relayed_refl.astype(jnp.float32)
    transmit = jnp.sqrt(1.0 - refl_full * refl_full) * jnp.exp(-relayed_decay.astype(jnp.float32))
    modes_all = lax.all_gather(relayed_modes, "blk", axis=2, tiled=True)
    modes_wide = modes_all.astype(jnp.float32)
    scaled_refl = (modes_wide * refl_full[:, None, :]).astype(jnp.bfloat16)
    scaled_tran = (modes_wide * transmit[:, None, :]).astype(jnp.bfloat16)
    refl_blk = jnp.einsum(
        "lhm,lkm->lhk", modes_all, scaled_refl, preferred_element_type=jnp.float32
    ).astype(jnp.bfloat16)
    tran_blk = jnp.einsum(
        "lhm,lkm->lhk", modes_all, scaled_tran, preferred_element_type=jnp.float32
    ).astype(jnp.bfloat16)
    layer_s = jnp.stack([refl_blk, tran_blk, tran_blk, -refl_blk], axis=1)
    row_count = HARM // block_count
    own_top, own_bottom = first_call(block_index, row_count, layer_s[0], layer_s[1])
    group_index = lax.axis_index("layer")
    level_count = lax.axis_size("layer").bit_length() - 1
    for section_level in range(level_count):
        distance = 1 << section_level
        lower_far = spread(own_bottom, "blk")
        upper_top = passed_along(own_top, "layer", distance)
        upper_top, later_bottom = lax.optimization_barrier([upper_top, own_bottom])
        upper_bottom = passed_along(later_bottom, "layer", distance)
        upper_far = spread(upper_top, "blk")
        own_top, own_bottom = level_call(
            group_index >= distance,
            block_index,
            upper_far,
            upper_bottom,
            lower_far,
            own_top,
            own_bottom,
        )
    own_rows = jnp.stack([own_bottom[1], own_bottom[0], own_top[1], own_top[0]])
    return own_rows[None]


def solution(mesh):
    placed = (P(None, "layer", "blk"), P(None, "layer"), P(None, "layer"))
    return jax.shard_map(
        on_device,
        mesh=mesh,
        in_specs=placed,
        out_specs=P("layer", None, "blk", None),
        check_vma=False,
    )
```

```python
import functools

import jax
import jax.numpy as jnp
from jax import lax
from jax.sharding import PartitionSpec as P
from jax.experimental import pallas as pl
from jax.experimental.pallas import tpu as pltpu

HARM = 512
REFL = 4


def passed_along(value, axis, steps):
    count = lax.axis_size(axis)
    first, last = (max(0, -steps), min(count, count - steps))
    return lax.ppermute(value, axis, [(source, source + steps) for source in range(first, last)])


def rotated(value, axis, steps):
    count = lax.axis_size(axis)
    return lax.ppermute(value, axis, [(source, (source + steps) % count) for source in range(count)])


def times_f32(left_op, right_op):
    return jnp.dot(left_op, right_op, preferred_element_type=jnp.float32)


def star_whole(upper_s, lower_s):
    coupling_down = times_f32(lower_s[0], upper_s[3]).astype(jnp.bfloat16)
    coupling_up = times_f32(upper_s[3], lower_s[0]).astype(jnp.bfloat16)
    left_sum = upper_s[1]
    for repeat in range(REFL):
        left_sum = (upper_s[1] + times_f32(left_sum, coupling_down)).astype(jnp.bfloat16)
    right_sum = lower_s[2]
    for repeat in range(REFL):
        right_sum = (lower_s[2] + times_f32(right_sum, coupling_up)).astype(jnp.bfloat16)
    left_mid = times_f32(left_sum, lower_s[0]).astype(jnp.bfloat16)
    right_mid = times_f32(right_sum, upper_s[3]).astype(jnp.bfloat16)
    new_refl = (upper_s[0] + times_f32(left_mid, upper_s[2])).astype(jnp.bfloat16)
    new_back = times_f32(left_sum, lower_s[1]).astype(jnp.bfloat16)
    new_fore = times_f32(right_sum, upper_s[2]).astype(jnp.bfloat16)
    new_under = (lower_s[3] + times_f32(right_mid, lower_s[1])).astype(jnp.bfloat16)
    return [new_refl, new_back, new_fore, new_under]


def assembled(pieces_ref, slot, own_piece):
    piece_count = pieces_ref.shape[0]
    return jnp.concatenate(
        [
            pieces_ref[(own_piece - source + piece_count) % piece_count, slot]
            for source in range(piece_count)
        ],
        axis=0,
    )


def first_kernel(ctl_ref, upper_ref, lower_ref, top_ref, bottom_ref, whole_ref):
    own_piece = ctl_ref[0]
    row_count = top_ref.shape[1]
    new_s = star_whole(
        [upper_ref[block] for block in range(4)], [lower_ref[block] for block in range(4)]
    )
    for block in range(4):
        whole_ref[block] = new_s[block]
    row_start = pl.multiple_of(own_piece * row_count, row_count)
    for slot, block in enumerate((3, 2)):
        top_ref[slot] = whole_ref[block, pl.ds(row_start, row_count), :]
    for slot, block in enumerate((1, 0)):
        bottom_ref[slot] = whole_ref[block, pl.ds(row_start, row_count), :]


def level_kernel(ctl_ref, *refs):
    moved_refs = refs[:-6]
    near_ref, top_ref, bottom_ref, new_top_ref, new_bottom_ref, whole_ref = refs[-6:]
    piece_count = len(moved_refs)
    row_count = near_ref.shape[1]
    active = ctl_ref[0]
    own_piece = ctl_ref[1]

    @pl.when(active == 0)
    def _keep():
        new_top_ref[...] = top_ref[...]
        new_bottom_ref[...] = bottom_ref[...]

    for position in range(piece_count):

        @pl.when((active != 0) & (own_piece == position))
        def _place():
            for shift, moved_ref in enumerate(moved_refs):
                source = (position - shift) % piece_count
                whole_ref[:, source * row_count : (source + 1) * row_count, :] = moved_ref[...]

    @pl.when(active != 0)
    def _combine():
        a22 = whole_ref[0]
        a21 = whole_ref[1]
        b12 = whole_ref[2]
        b11 = whole_ref[3]
        a12 = near_ref[0]
        a11 = near_ref[1]
        b22 = top_ref[0]
        b21 = top_ref[1]
        coupling_down = times_f32(b11, a22).astype(jnp.bfloat16)
        coupling_up = times_f32(a22, b11).astype(jnp.bfloat16)
        left_sum = a12
        for repeat in range(REFL):
            left_sum = (a12 + times_f32(left_sum, coupling_down)).astype(jnp.bfloat16)
        right_sum = b21
        for repeat in range(REFL):
            right_sum = (b21 + times_f32(right_sum, coupling_up)).astype(jnp.bfloat16)
        left_mid = times_f32(left_sum, b11).astype(jnp.bfloat16)
        right_mid = times_f32(right_sum, a22).astype(jnp.bfloat16)
        new_bottom_ref[1] = (a11 + times_f32(left_mid, a21)).astype(jnp.bfloat16)
        new_bottom_ref[0] = times_f32(left_sum, b12).astype(jnp.bfloat16)
        new_top_ref[1] = times_f32(right_sum, a21).astype(jnp.bfloat16)
        new_top_ref[0] = (b22 + times_f32(right_mid, b12)).astype(jnp.bfloat16)


def first_call(own_piece, row_count, upper_s, lower_s):
    ctl = own_piece.astype(jnp.int32).reshape(1)
    row_shape = jax.ShapeDtypeStruct((2, row_count, lower_s.shape[2]), lower_s.dtype)
    vmem = pl.BlockSpec(memory_space=pltpu.VMEM)
    return pl.pallas_call(
        first_kernel,
        out_shape=(row_shape, row_shape),
        in_specs=[pl.BlockSpec(memory_space=pltpu.SMEM), vmem, vmem],
        out_specs=(vmem, vmem),
        scratch_shapes=[pltpu.VMEM(lower_s.shape, lower_s.dtype)],
    )(ctl, upper_s, lower_s)


def level_call(active, own_piece, moved, near, top, bottom):
    ctl = jnp.stack([active.astype(jnp.int32), own_piece.astype(jnp.int32)])
    row_shape = jax.ShapeDtypeStruct(top.shape, top.dtype)
    whole_shape = (moved[0].shape[0], moved[0].shape[1] * len(moved), moved[0].shape[2])
    vmem = pl.BlockSpec(memory_space=pltpu.VMEM)
    return pl.pallas_call(
        level_kernel,
        out_shape=(row_shape, row_shape),
        in_specs=[pl.BlockSpec(memory_space=pltpu.SMEM)] + [vmem] * (len(moved) + 3),
        out_specs=(vmem, vmem),
        scratch_shapes=[pltpu.VMEM(whole_shape, top.dtype)],
    )(ctl, *moved, near, top, bottom)


def on_device(mode_matrix, decay_rate, facet_refl):
    coefficients = jnp.stack([decay_rate, facet_refl], axis=-1)
    relayed_modes = lax.all_to_all(mode_matrix, "layer", split_axis=0, concat_axis=1, tiled=True)
    relayed_coeff = lax.all_to_all(coefficients, "layer", split_axis=0, concat_axis=1, tiled=True)
    relayed_decay = relayed_coeff[..., 0]
    relayed_refl = relayed_coeff[..., 1]
    block_index = lax.axis_index("blk")
    block_count = lax.axis_size("blk")
    refl_full = relayed_refl.astype(jnp.float32)
    transmit = jnp.sqrt(1.0 - refl_full * refl_full) * jnp.exp(-relayed_decay.astype(jnp.float32))
    modes_all = lax.all_gather(relayed_modes, "blk", axis=2, tiled=True)
    modes_wide = modes_all.astype(jnp.float32)
    scaled_refl = (modes_wide * refl_full[:, None, :]).astype(jnp.bfloat16)
    scaled_tran = (modes_wide * transmit[:, None, :]).astype(jnp.bfloat16)
    refl_blk = jnp.einsum(
        "lhm,lkm->lhk", modes_all, scaled_refl, preferred_element_type=jnp.float32
    ).astype(jnp.bfloat16)
    tran_blk = jnp.einsum(
        "lhm,lkm->lhk", modes_all, scaled_tran, preferred_element_type=jnp.float32
    ).astype(jnp.bfloat16)
    layer_s = jnp.stack([refl_blk, tran_blk, tran_blk, -refl_blk], axis=1)
    row_count = HARM // block_count
    own_top, own_bottom = first_call(block_index, row_count, layer_s[0], layer_s[1])
    group_index = lax.axis_index("layer")
    level_count = lax.axis_size("layer").bit_length() - 1
    for section_level in range(level_count):
        distance = 1 << section_level
        upper_top = passed_along(own_top, "layer", distance)
        upper_top, later_bottom = lax.optimization_barrier([upper_top, own_bottom])
        upper_bottom = passed_along(later_bottom, "layer", distance)
        far_rows = jnp.concatenate([upper_top, own_bottom])
        moved = [far_rows] + [rotated(far_rows, "blk", shift) for shift in range(1, block_count)]
        own_top, own_bottom = level_call(
            group_index >= distance, block_index, moved, upper_bottom, own_top, own_bottom
        )
    own_rows = jnp.stack([own_bottom[1], own_bottom[0], own_top[1], own_top[0]])
    return own_rows[None]


def solution(mesh):
    placed = (P(None, "layer", "blk"), P(None, "layer"), P(None, "layer"))
    return jax.shard_map(
        on_device,
        mesh=mesh,
        in_specs=placed,
        out_specs=P("layer", None, "blk", None),
        check_vma=False,
    )
```

```python
import functools

import jax
import jax.numpy as jnp
from jax import lax
from jax.sharding import PartitionSpec as P
from jax.experimental import pallas as pl
from jax.experimental.pallas import tpu as pltpu

HARM = 512
REFL = 4


def passed_along(value, axis, steps):
    count = lax.axis_size(axis)
    first, last = (max(0, -steps), min(count, count - steps))
    return lax.ppermute(value, axis, [(source, source + steps) for source in range(first, last)])


def rotated(value, axis, steps):
    count = lax.axis_size(axis)
    return lax.ppermute(value, axis, [(source, (source + steps) % count) for source in range(count)])


def times_f32(left_op, right_op):
    return jnp.dot(left_op, right_op, preferred_element_type=jnp.float32)


def star_whole(upper_s, lower_s):
    coupling_down = times_f32(lower_s[0], upper_s[3]).astype(jnp.bfloat16)
    coupling_up = times_f32(upper_s[3], lower_s[0]).astype(jnp.bfloat16)
    left_sum = upper_s[1]
    for repeat in range(REFL):
        left_sum = (upper_s[1] + times_f32(left_sum, coupling_down)).astype(jnp.bfloat16)
    right_sum = lower_s[2]
    for repeat in range(REFL):
        right_sum = (lower_s[2] + times_f32(right_sum, coupling_up)).astype(jnp.bfloat16)
    left_mid = times_f32(left_sum, lower_s[0]).astype(jnp.bfloat16)
    right_mid = times_f32(right_sum, upper_s[3]).astype(jnp.bfloat16)
    new_refl = (upper_s[0] + times_f32(left_mid, upper_s[2])).astype(jnp.bfloat16)
    new_back = times_f32(left_sum, lower_s[1]).astype(jnp.bfloat16)
    new_fore = times_f32(right_sum, upper_s[2]).astype(jnp.bfloat16)
    new_under = (lower_s[3] + times_f32(right_mid, lower_s[1])).astype(jnp.bfloat16)
    return [new_refl, new_back, new_fore, new_under]


def assembled(pieces_ref, slot, own_piece):
    piece_count = pieces_ref.shape[0]
    return jnp.concatenate(
        [
            pieces_ref[(own_piece - source + piece_count) % piece_count, slot]
            for source in range(piece_count)
        ],
        axis=0,
    )


def first_kernel(ctl_ref, upper_ref, lower_ref, top_ref, bottom_ref, whole_ref):
    own_piece = ctl_ref[0]
    row_count = top_ref.shape[1]
    new_s = star_whole(
        [upper_ref[block] for block in range(4)], [lower_ref[block] for block in range(4)]
    )
    for block in range(4):
        whole_ref[block] = new_s[block]
    row_start = pl.multiple_of(own_piece * row_count, row_count)
    for slot, block in enumerate((3, 2)):
        top_ref[slot] = whole_ref[block, pl.ds(row_start, row_count), :]
    for slot, block in enumerate((1, 0)):
        bottom_ref[slot] = whole_ref[block, pl.ds(row_start, row_count), :]


def level_kernel(ctl_ref, *refs):
    piece_count = (len(refs) - 6) // 2
    far_refs, low_refs = refs[:piece_count], refs[piece_count : 2 * piece_count]
    near_ref, top_ref, bottom_ref, new_top_ref, new_bottom_ref, whole_ref = refs[-6:]
    row_count = near_ref.shape[1]
    active = ctl_ref[0]
    own_piece = ctl_ref[1]

    @pl.when(active == 0)
    def _keep():
        new_top_ref[...] = top_ref[...]
        new_bottom_ref[...] = bottom_ref[...]

    for position in range(piece_count):

        @pl.when((active != 0) & (own_piece == position))
        def _place():
            for shift in range(piece_count):
                rows = slice(((position - shift) % piece_count) * row_count, None)
                rows = slice(rows.start, rows.start + row_count)
                whole_ref[0:2, rows, :] = far_refs[shift][...]
                whole_ref[2:4, rows, :] = low_refs[shift][...]

    @pl.when(active != 0)
    def _combine():
        a22 = whole_ref[0]
        a21 = whole_ref[1]
        b12 = whole_ref[2]
        b11 = whole_ref[3]
        a12 = near_ref[0]
        a11 = near_ref[1]
        b22 = top_ref[0]
        b21 = top_ref[1]
        coupling_down = times_f32(b11, a22).astype(jnp.bfloat16)
        coupling_up = times_f32(a22, b11).astype(jnp.bfloat16)
        left_sum = a12
        for repeat in range(REFL):
            left_sum = (a12 + times_f32(left_sum, coupling_down)).astype(jnp.bfloat16)
        right_sum = b21
        for repeat in range(REFL):
            right_sum = (b21 + times_f32(right_sum, coupling_up)).astype(jnp.bfloat16)
        left_mid = times_f32(left_sum, b11).astype(jnp.bfloat16)
        right_mid = times_f32(right_sum, a22).astype(jnp.bfloat16)
        new_bottom_ref[1] = (a11 + times_f32(left_mid, a21)).astype(jnp.bfloat16)
        new_bottom_ref[0] = times_f32(left_sum, b12).astype(jnp.bfloat16)
        new_top_ref[1] = times_f32(right_sum, a21).astype(jnp.bfloat16)
        new_top_ref[0] = (b22 + times_f32(right_mid, b12)).astype(jnp.bfloat16)


def first_call(own_piece, row_count, upper_s, lower_s):
    ctl = own_piece.astype(jnp.int32).reshape(1)
    row_shape = jax.ShapeDtypeStruct((2, row_count, lower_s.shape[2]), lower_s.dtype)
    vmem = pl.BlockSpec(memory_space=pltpu.VMEM)
    return pl.pallas_call(
        first_kernel,
        out_shape=(row_shape, row_shape),
        in_specs=[pl.BlockSpec(memory_space=pltpu.SMEM), vmem, vmem],
        out_specs=(vmem, vmem),
        scratch_shapes=[pltpu.VMEM(lower_s.shape, lower_s.dtype)],
    )(ctl, upper_s, lower_s)


def level_call(active, own_piece, far, low, near, top, bottom):
    ctl = jnp.stack([active.astype(jnp.int32), own_piece.astype(jnp.int32)])
    row_shape = jax.ShapeDtypeStruct(top.shape, top.dtype)
    whole_shape = (4, far[0].shape[1] * len(far), far[0].shape[2])
    vmem = pl.BlockSpec(memory_space=pltpu.VMEM)
    return pl.pallas_call(
        level_kernel,
        out_shape=(row_shape, row_shape),
        in_specs=[pl.BlockSpec(memory_space=pltpu.SMEM)] + [vmem] * (2 * len(far) + 3),
        out_specs=(vmem, vmem),
        scratch_shapes=[pltpu.VMEM(whole_shape, top.dtype)],
    )(ctl, *far, *low, near, top, bottom)


def spread(value, axis):
    count = lax.axis_size(axis)
    return [value] + [rotated(value, axis, shift) for shift in range(1, count)]


def on_device(mode_matrix, decay_rate, facet_refl):
    coefficients = jnp.stack([decay_rate, facet_refl], axis=-1)
    relayed_modes = lax.all_to_all(mode_matrix, "layer", split_axis=0, concat_axis=1, tiled=True)
    relayed_coeff = lax.all_to_all(coefficients, "layer", split_axis=0, concat_axis=1, tiled=True)
    relayed_decay = relayed_coeff[..., 0]
    relayed_refl = relayed_coeff[..., 1]
    block_index = lax.axis_index("blk")
    block_count = lax.axis_size("blk")
    refl_full = relayed_refl.astype(jnp.float32)
    transmit = jnp.sqrt(1.0 - refl_full * refl_full) * jnp.exp(-relayed_decay.astype(jnp.float32))
    modes_all = lax.all_gather(relayed_modes, "blk", axis=2, tiled=True)
    modes_wide = modes_all.astype(jnp.float32)
    scaled_refl = (modes_wide * refl_full[:, None, :]).astype(jnp.bfloat16)
    scaled_tran = (modes_wide * transmit[:, None, :]).astype(jnp.bfloat16)
    refl_blk = jnp.einsum(
        "lhm,lkm->lhk", modes_all, scaled_refl, preferred_element_type=jnp.float32
    ).astype(jnp.bfloat16)
    tran_blk = jnp.einsum(
        "lhm,lkm->lhk", modes_all, scaled_tran, preferred_element_type=jnp.float32
    ).astype(jnp.bfloat16)
    layer_s = jnp.stack([refl_blk, tran_blk, tran_blk, -refl_blk], axis=1)
    row_count = HARM // block_count
    own_top, own_bottom = first_call(block_index, row_count, layer_s[0], layer_s[1])
    group_index = lax.axis_index("layer")
    level_count = lax.axis_size("layer").bit_length() - 1
    for section_level in range(level_count):
        distance = 1 << section_level
        lower_far = spread(own_bottom, "blk")
        upper_top = passed_along(own_top, "layer", distance)
        upper_top, later_bottom = lax.optimization_barrier([upper_top, own_bottom])
        upper_bottom = passed_along(later_bottom, "layer", distance)
        upper_far = spread(upper_top, "blk")
        own_top, own_bottom = level_call(
            group_index >= distance,
            block_index,
            upper_far,
            lower_far,
            upper_bottom,
            own_top,
            own_bottom,
        )
    own_rows = jnp.stack([own_bottom[1], own_bottom[0], own_top[1], own_top[0]])
    return own_rows[None]


def solution(mesh):
    placed = (P(None, "layer", "blk"), P(None, "layer"), P(None, "layer"))
    return jax.shard_map(
        on_device,
        mesh=mesh,
        in_specs=placed,
        out_specs=P("layer", None, "blk", None),
        check_vma=False,
    )
```

```python
import functools

import jax
import jax.numpy as jnp
from jax import lax
from jax.sharding import PartitionSpec as P
from jax.experimental import pallas as pl
from jax.experimental.pallas import tpu as pltpu

HARM = 512
REFL = 4


def passed_along(value, axis, steps):
    count = lax.axis_size(axis)
    first, last = (max(0, -steps), min(count, count - steps))
    return lax.ppermute(value, axis, [(source, source + steps) for source in range(first, last)])


def rotated(value, axis, steps):
    count = lax.axis_size(axis)
    return lax.ppermute(value, axis, [(source, (source + steps) % count) for source in range(count)])


def times_f32(left_op, right_op):
    return jnp.dot(left_op, right_op, preferred_element_type=jnp.float32)


def star_whole(upper_s, lower_s):
    coupling_down = times_f32(lower_s[0], upper_s[3]).astype(jnp.bfloat16)
    coupling_up = times_f32(upper_s[3], lower_s[0]).astype(jnp.bfloat16)
    left_sum = upper_s[1]
    for repeat in range(REFL):
        left_sum = (upper_s[1] + times_f32(left_sum, coupling_down)).astype(jnp.bfloat16)
    right_sum = lower_s[2]
    for repeat in range(REFL):
        right_sum = (lower_s[2] + times_f32(right_sum, coupling_up)).astype(jnp.bfloat16)
    left_mid = times_f32(left_sum, lower_s[0]).astype(jnp.bfloat16)
    right_mid = times_f32(right_sum, upper_s[3]).astype(jnp.bfloat16)
    new_refl = (upper_s[0] + times_f32(left_mid, upper_s[2])).astype(jnp.bfloat16)
    new_back = times_f32(left_sum, lower_s[1]).astype(jnp.bfloat16)
    new_fore = times_f32(right_sum, upper_s[2]).astype(jnp.bfloat16)
    new_under = (lower_s[3] + times_f32(right_mid, lower_s[1])).astype(jnp.bfloat16)
    return [new_refl, new_back, new_fore, new_under]


def assembled(pieces_ref, slot, own_piece):
    piece_count = pieces_ref.shape[0]
    return jnp.concatenate(
        [
            pieces_ref[(own_piece - source + piece_count) % piece_count, slot]
            for source in range(piece_count)
        ],
        axis=0,
    )


def first_kernel(ctl_ref, upper_ref, lower_ref, top_ref, bottom_ref, whole_ref):
    own_piece = ctl_ref[0]
    row_count = top_ref.shape[1]
    new_s = star_whole(
        [upper_ref[block] for block in range(4)], [lower_ref[block] for block in range(4)]
    )
    for block in range(4):
        whole_ref[block] = new_s[block]
    row_start = pl.multiple_of(own_piece * row_count, row_count)
    for slot, block in enumerate((3, 2)):
        top_ref[slot] = whole_ref[block, pl.ds(row_start, row_count), :]
    for slot, block in enumerate((1, 0)):
        bottom_ref[slot] = whole_ref[block, pl.ds(row_start, row_count), :]


def level_kernel(ctl_ref, *refs):
    far_refs, low_refs = refs[:1], refs[1:2]
    piece_count = far_refs[0].shape[0]
    near_ref, top_ref, bottom_ref, new_top_ref, new_bottom_ref, whole_ref = refs[-6:]
    row_count = near_ref.shape[1]
    active = ctl_ref[0]
    own_piece = ctl_ref[1]

    @pl.when(active == 0)
    def _keep():
        new_top_ref[...] = top_ref[...]
        new_bottom_ref[...] = bottom_ref[...]

    @pl.when(active != 0)
    def _place():
        for source in range(piece_count):
            rows = slice(source * row_count, (source + 1) * row_count)
            whole_ref[0:2, rows, :] = far_refs[0][source]
            whole_ref[2:4, rows, :] = low_refs[0][source]

    @pl.when(active != 0)
    def _combine():
        a22 = whole_ref[0]
        a21 = whole_ref[1]
        b12 = whole_ref[2]
        b11 = whole_ref[3]
        a12 = near_ref[0]
        a11 = near_ref[1]
        b22 = top_ref[0]
        b21 = top_ref[1]
        coupling_down = times_f32(b11, a22).astype(jnp.bfloat16)
        coupling_up = times_f32(a22, b11).astype(jnp.bfloat16)
        left_sum = a12
        for repeat in range(REFL):
            left_sum = (a12 + times_f32(left_sum, coupling_down)).astype(jnp.bfloat16)
        right_sum = b21
        for repeat in range(REFL):
            right_sum = (b21 + times_f32(right_sum, coupling_up)).astype(jnp.bfloat16)
        left_mid = times_f32(left_sum, b11).astype(jnp.bfloat16)
        right_mid = times_f32(right_sum, a22).astype(jnp.bfloat16)
        new_bottom_ref[1] = (a11 + times_f32(left_mid, a21)).astype(jnp.bfloat16)
        new_bottom_ref[0] = times_f32(left_sum, b12).astype(jnp.bfloat16)
        new_top_ref[1] = times_f32(right_sum, a21).astype(jnp.bfloat16)
        new_top_ref[0] = (b22 + times_f32(right_mid, b12)).astype(jnp.bfloat16)


def first_call(own_piece, row_count, upper_s, lower_s):
    ctl = own_piece.astype(jnp.int32).reshape(1)
    row_shape = jax.ShapeDtypeStruct((2, row_count, lower_s.shape[2]), lower_s.dtype)
    vmem = pl.BlockSpec(memory_space=pltpu.VMEM)
    return pl.pallas_call(
        first_kernel,
        out_shape=(row_shape, row_shape),
        in_specs=[pl.BlockSpec(memory_space=pltpu.SMEM), vmem, vmem],
        out_specs=(vmem, vmem),
        scratch_shapes=[pltpu.VMEM(lower_s.shape, lower_s.dtype)],
    )(ctl, upper_s, lower_s)


def level_call(active, own_piece, far, low, near, top, bottom):
    ctl = jnp.stack([active.astype(jnp.int32), own_piece.astype(jnp.int32)])
    row_shape = jax.ShapeDtypeStruct(top.shape, top.dtype)
    whole_shape = (4, far.shape[2] * far.shape[0], far.shape[3])
    vmem = pl.BlockSpec(memory_space=pltpu.VMEM)
    return pl.pallas_call(
        level_kernel,
        out_shape=(row_shape, row_shape),
        in_specs=[pl.BlockSpec(memory_space=pltpu.SMEM)] + [vmem] * 5,
        out_specs=(vmem, vmem),
        scratch_shapes=[pltpu.VMEM(whole_shape, top.dtype)],
    )(ctl, far, low, near, top, bottom)


def spread(value, axis):
    count = lax.axis_size(axis)
    copies = jnp.broadcast_to(value[None], (count,) + value.shape)
    return lax.all_to_all(copies, axis, split_axis=0, concat_axis=0, tiled=True)


def on_device(mode_matrix, decay_rate, facet_refl):
    coefficients = jnp.stack([decay_rate, facet_refl], axis=-1)
    relayed_modes = lax.all_to_all(mode_matrix, "layer", split_axis=0, concat_axis=1, tiled=True)
    relayed_coeff = lax.all_to_all(coefficients, "layer", split_axis=0, concat_axis=1, tiled=True)
    relayed_decay = relayed_coeff[..., 0]
    relayed_refl = relayed_coeff[..., 1]
    block_index = lax.axis_index("blk")
    block_count = lax.axis_size("blk")
    refl_full = relayed_refl.astype(jnp.float32)
    transmit = jnp.sqrt(1.0 - refl_full * refl_full) * jnp.exp(-relayed_decay.astype(jnp.float32))
    modes_all = lax.all_gather(relayed_modes, "blk", axis=2, tiled=True)
    modes_wide = modes_all.astype(jnp.float32)
    scaled_refl = (modes_wide * refl_full[:, None, :]).astype(jnp.bfloat16)
    scaled_tran = (modes_wide * transmit[:, None, :]).astype(jnp.bfloat16)
    refl_blk = jnp.einsum(
        "lhm,lkm->lhk", modes_all, scaled_refl, preferred_element_type=jnp.float32
    ).astype(jnp.bfloat16)
    tran_blk = jnp.einsum(
        "lhm,lkm->lhk", modes_all, scaled_tran, preferred_element_type=jnp.float32
    ).astype(jnp.bfloat16)
    layer_s = jnp.stack([refl_blk, tran_blk, tran_blk, -refl_blk], axis=1)
    row_count = HARM // block_count
    own_top, own_bottom = first_call(block_index, row_count, layer_s[0], layer_s[1])
    group_index = lax.axis_index("layer")
    level_count = lax.axis_size("layer").bit_length() - 1
    for section_level in range(level_count):
        distance = 1 << section_level
        lower_far = spread(own_bottom, "blk")
        upper_top = passed_along(own_top, "layer", distance)
        upper_top, later_bottom = lax.optimization_barrier([upper_top, own_bottom])
        upper_bottom = passed_along(later_bottom, "layer", distance)
        upper_far = spread(upper_top, "blk")
        own_top, own_bottom = level_call(
            group_index >= distance,
            block_index,
            upper_far,
            lower_far,
            upper_bottom,
            own_top,
            own_bottom,
        )
    own_rows = jnp.stack([own_bottom[1], own_bottom[0], own_top[1], own_top[0]])
    return own_rows[None]


def solution(mesh):
    placed = (P(None, "layer", "blk"), P(None, "layer"), P(None, "layer"))
    return jax.shard_map(
        on_device,
        mesh=mesh,
        in_specs=placed,
        out_specs=P("layer", None, "blk", None),
        check_vma=False,
    )
```

```python
import functools

import jax
import jax.numpy as jnp
from jax import lax
from jax.sharding import PartitionSpec as P
from jax.experimental import pallas as pl
from jax.experimental.pallas import tpu as pltpu

HARM = 512
REFL = 4


def passed_along(value, axis, steps):
    count = lax.axis_size(axis)
    first, last = (max(0, -steps), min(count, count - steps))
    return lax.ppermute(value, axis, [(source, source + steps) for source in range(first, last)])


def rotated(value, axis, steps):
    count = lax.axis_size(axis)
    return lax.ppermute(value, axis, [(source, (source + steps) % count) for source in range(count)])


def times_f32(left_op, right_op):
    return jnp.dot(left_op, right_op, preferred_element_type=jnp.float32)


def star_whole(upper_s, lower_s):
    coupling_down = times_f32(lower_s[0], upper_s[3]).astype(jnp.bfloat16)
    coupling_up = times_f32(upper_s[3], lower_s[0]).astype(jnp.bfloat16)
    left_sum = upper_s[1]
    for repeat in range(REFL):
        left_sum = (upper_s[1] + times_f32(left_sum, coupling_down)).astype(jnp.bfloat16)
    right_sum = lower_s[2]
    for repeat in range(REFL):
        right_sum = (lower_s[2] + times_f32(right_sum, coupling_up)).astype(jnp.bfloat16)
    left_mid = times_f32(left_sum, lower_s[0]).astype(jnp.bfloat16)
    right_mid = times_f32(right_sum, upper_s[3]).astype(jnp.bfloat16)
    new_refl = (upper_s[0] + times_f32(left_mid, upper_s[2])).astype(jnp.bfloat16)
    new_back = times_f32(left_sum, lower_s[1]).astype(jnp.bfloat16)
    new_fore = times_f32(right_sum, upper_s[2]).astype(jnp.bfloat16)
    new_under = (lower_s[3] + times_f32(right_mid, lower_s[1])).astype(jnp.bfloat16)
    return [new_refl, new_back, new_fore, new_under]


def assembled(pieces_ref, slot, own_piece):
    piece_count = pieces_ref.shape[0]
    return jnp.concatenate(
        [
            pieces_ref[(own_piece - source + piece_count) % piece_count, slot]
            for source in range(piece_count)
        ],
        axis=0,
    )


def first_kernel(ctl_ref, upper_ref, lower_ref, top_ref, bottom_ref, whole_ref):
    own_piece = ctl_ref[0]
    row_count = top_ref.shape[1]
    new_s = star_whole(
        [upper_ref[block] for block in range(4)], [lower_ref[block] for block in range(4)]
    )
    for block in range(4):
        whole_ref[block] = new_s[block]
    row_start = pl.multiple_of(own_piece * row_count, row_count)
    for slot, block in enumerate((3, 2)):
        top_ref[slot] = whole_ref[block, pl.ds(row_start, row_count), :]
    for slot, block in enumerate((1, 0)):
        bottom_ref[slot] = whole_ref[block, pl.ds(row_start, row_count), :]


def level_kernel(ctl_ref, *refs):
    piece_count = (len(refs) - 6) // 2
    far_refs, low_refs = refs[:piece_count], refs[piece_count : 2 * piece_count]
    near_ref, top_ref, bottom_ref, new_top_ref, new_bottom_ref, whole_ref = refs[-6:]
    row_count = near_ref.shape[1]
    active = ctl_ref[0]
    own_piece = ctl_ref[1]

    @pl.when(active == 0)
    def _keep():
        new_top_ref[...] = top_ref[...]
        new_bottom_ref[...] = bottom_ref[...]

    for position in range(piece_count):

        @pl.when((active != 0) & (own_piece == position))
        def _place():
            for shift in range(piece_count):
                rows = slice(((position - shift) % piece_count) * row_count, None)
                rows = slice(rows.start, rows.start + row_count)
                whole_ref[0:2, rows, :] = far_refs[shift][...]
                whole_ref[2:4, rows, :] = low_refs[shift][...]

    @pl.when(active != 0)
    def _combine():
        a22 = whole_ref[0]
        a21 = whole_ref[1]
        b12 = whole_ref[2]
        b11 = whole_ref[3]
        a12 = near_ref[0]
        a11 = near_ref[1]
        b22 = top_ref[0]
        b21 = top_ref[1]
        coupling_down = times_f32(b11, a22).astype(jnp.bfloat16)
        coupling_up = times_f32(a22, b11).astype(jnp.bfloat16)
        left_sum = a12
        for repeat in range(REFL):
            left_sum = (a12 + times_f32(left_sum, coupling_down)).astype(jnp.bfloat16)
        right_sum = b21
        for repeat in range(REFL):
            right_sum = (b21 + times_f32(right_sum, coupling_up)).astype(jnp.bfloat16)
        left_mid = times_f32(left_sum, b11).astype(jnp.bfloat16)
        right_mid = times_f32(right_sum, a22).astype(jnp.bfloat16)
        new_bottom_ref[1] = (a11 + times_f32(left_mid, a21)).astype(jnp.bfloat16)
        new_bottom_ref[0] = times_f32(left_sum, b12).astype(jnp.bfloat16)
        new_top_ref[1] = times_f32(right_sum, a21).astype(jnp.bfloat16)
        new_top_ref[0] = (b22 + times_f32(right_mid, b12)).astype(jnp.bfloat16)


def first_call(own_piece, row_count, upper_s, lower_s):
    ctl = own_piece.astype(jnp.int32).reshape(1)
    row_shape = jax.ShapeDtypeStruct((2, row_count, lower_s.shape[2]), lower_s.dtype)
    vmem = pl.BlockSpec(memory_space=pltpu.VMEM)
    return pl.pallas_call(
        first_kernel,
        out_shape=(row_shape, row_shape),
        in_specs=[pl.BlockSpec(memory_space=pltpu.SMEM), vmem, vmem],
        out_specs=(vmem, vmem),
        scratch_shapes=[pltpu.VMEM(lower_s.shape, lower_s.dtype)],
    )(ctl, upper_s, lower_s)


def level_call(active, own_piece, far, low, near, top, bottom):
    ctl = jnp.stack([active.astype(jnp.int32), own_piece.astype(jnp.int32)])
    row_shape = jax.ShapeDtypeStruct(top.shape, top.dtype)
    whole_shape = (4, far[0].shape[1] * len(far), far[0].shape[2])
    vmem = pl.BlockSpec(memory_space=pltpu.VMEM)
    return pl.pallas_call(
        level_kernel,
        out_shape=(row_shape, row_shape),
        in_specs=[pl.BlockSpec(memory_space=pltpu.SMEM)] + [vmem] * (2 * len(far) + 3),
        out_specs=(vmem, vmem),
        scratch_shapes=[pltpu.VMEM(whole_shape, top.dtype)],
    )(ctl, *far, *low, near, top, bottom)


def spread(value, axis):
    count = lax.axis_size(axis)
    return [value] + [rotated(value, axis, shift) for shift in range(1, count)]


def on_device(mode_matrix, decay_rate, facet_refl):
    coefficients = jnp.stack([decay_rate, facet_refl], axis=-1)
    every_coeff = lax.all_gather(coefficients, "layer", axis=1, tiled=True)
    relayed_modes = lax.all_to_all(mode_matrix, "layer", split_axis=0, concat_axis=1, tiled=True)
    layers_here = relayed_modes.shape[0]
    relayed_coeff = lax.dynamic_slice_in_dim(
        every_coeff, lax.axis_index("layer") * layers_here, layers_here, 0
    )
    relayed_decay = relayed_coeff[..., 0]
    relayed_refl = relayed_coeff[..., 1]
    block_index = lax.axis_index("blk")
    block_count = lax.axis_size("blk")
    refl_full = relayed_refl.astype(jnp.float32)
    transmit = jnp.sqrt(1.0 - refl_full * refl_full) * jnp.exp(-relayed_decay.astype(jnp.float32))
    modes_all = lax.all_gather(relayed_modes, "blk", axis=2, tiled=True)
    modes_wide = modes_all.astype(jnp.float32)
    scaled_refl = (modes_wide * refl_full[:, None, :]).astype(jnp.bfloat16)
    scaled_tran = (modes_wide * transmit[:, None, :]).astype(jnp.bfloat16)
    refl_blk = jnp.einsum(
        "lhm,lkm->lhk", modes_all, scaled_refl, preferred_element_type=jnp.float32
    ).astype(jnp.bfloat16)
    tran_blk = jnp.einsum(
        "lhm,lkm->lhk", modes_all, scaled_tran, preferred_element_type=jnp.float32
    ).astype(jnp.bfloat16)
    layer_s = jnp.stack([refl_blk, tran_blk, tran_blk, -refl_blk], axis=1)
    row_count = HARM // block_count
    own_top, own_bottom = first_call(block_index, row_count, layer_s[0], layer_s[1])
    group_index = lax.axis_index("layer")
    level_count = lax.axis_size("layer").bit_length() - 1
    for section_level in range(level_count):
        distance = 1 << section_level
        lower_far = spread(own_bottom, "blk")
        upper_top = passed_along(own_top, "layer", distance)
        upper_top, later_bottom = lax.optimization_barrier([upper_top, own_bottom])
        upper_bottom = passed_along(later_bottom, "layer", distance)
        upper_far = spread(upper_top, "blk")
        own_top, own_bottom = level_call(
            group_index >= distance,
            block_index,
            upper_far,
            lower_far,
            upper_bottom,
            own_top,
            own_bottom,
        )
    own_rows = jnp.stack([own_bottom[1], own_bottom[0], own_top[1], own_top[0]])
    return own_rows[None]


def solution(mesh):
    placed = (P(None, "layer", "blk"), P(None, "layer"), P(None, "layer"))
    return jax.shard_map(
        on_device,
        mesh=mesh,
        in_specs=placed,
        out_specs=P("layer", None, "blk", None),
        check_vma=False,
    )
```

```python
import functools

import jax
import jax.numpy as jnp
from jax import lax
from jax.sharding import PartitionSpec as P
from jax.experimental import pallas as pl
from jax.experimental.pallas import tpu as pltpu

HARM = 512
REFL = 4


def passed_along(value, axis, steps):
    count = lax.axis_size(axis)
    first, last = (max(0, -steps), min(count, count - steps))
    return lax.ppermute(value, axis, [(source, source + steps) for source in range(first, last)])


def rotated(value, axis, steps):
    count = lax.axis_size(axis)
    return lax.ppermute(value, axis, [(source, (source + steps) % count) for source in range(count)])


def times_f32(left_op, right_op):
    return jnp.dot(left_op, right_op, preferred_element_type=jnp.float32)


def star_whole(upper_s, lower_s):
    coupling_down = times_f32(lower_s[0], upper_s[3]).astype(jnp.bfloat16)
    coupling_up = times_f32(upper_s[3], lower_s[0]).astype(jnp.bfloat16)
    left_sum = upper_s[1]
    for repeat in range(REFL):
        left_sum = (upper_s[1] + times_f32(left_sum, coupling_down)).astype(jnp.bfloat16)
    right_sum = lower_s[2]
    for repeat in range(REFL):
        right_sum = (lower_s[2] + times_f32(right_sum, coupling_up)).astype(jnp.bfloat16)
    left_mid = times_f32(left_sum, lower_s[0]).astype(jnp.bfloat16)
    right_mid = times_f32(right_sum, upper_s[3]).astype(jnp.bfloat16)
    new_refl = (upper_s[0] + times_f32(left_mid, upper_s[2])).astype(jnp.bfloat16)
    new_back = times_f32(left_sum, lower_s[1]).astype(jnp.bfloat16)
    new_fore = times_f32(right_sum, upper_s[2]).astype(jnp.bfloat16)
    new_under = (lower_s[3] + times_f32(right_mid, lower_s[1])).astype(jnp.bfloat16)
    return [new_refl, new_back, new_fore, new_under]


def assembled(pieces_ref, slot, own_piece):
    piece_count = pieces_ref.shape[0]
    return jnp.concatenate(
        [
            pieces_ref[(own_piece - source + piece_count) % piece_count, slot]
            for source in range(piece_count)
        ],
        axis=0,
    )


def star_rows(a11, a12, a21, a22, b11, b12, b21, b22):
    coupling_down = times_f32(b11, a22).astype(jnp.bfloat16)
    coupling_up = times_f32(a22, b11).astype(jnp.bfloat16)
    left_sum = a12
    for repeat in range(REFL):
        left_sum = (a12 + times_f32(left_sum, coupling_down)).astype(jnp.bfloat16)
    right_sum = b21
    for repeat in range(REFL):
        right_sum = (b21 + times_f32(right_sum, coupling_up)).astype(jnp.bfloat16)
    left_mid = times_f32(left_sum, b11).astype(jnp.bfloat16)
    right_mid = times_f32(right_sum, a22).astype(jnp.bfloat16)
    new_refl = (a11 + times_f32(left_mid, a21)).astype(jnp.bfloat16)
    new_back = times_f32(left_sum, b12).astype(jnp.bfloat16)
    new_fore = times_f32(right_sum, a21).astype(jnp.bfloat16)
    new_under = (b22 + times_f32(right_mid, b12)).astype(jnp.bfloat16)
    return new_refl, new_back, new_fore, new_under


def first_kernel(ctl_ref, modes_ref, scale_ref, top_ref, bottom_ref, whole_ref):
    own_piece = ctl_ref[0]
    row_count = top_ref.shape[1]
    for layer_pos in range(2):
        modes_one = modes_ref[layer_pos]
        modes_wide = modes_one.astype(jnp.float32)
        for kind in range(2):
            scaled = (modes_wide * scale_ref[layer_pos, kind]).astype(jnp.bfloat16)
            whole_ref[2 * layer_pos + kind] = lax.dot_general(
                modes_one,
                scaled,
                (((1,), (1,)), ((), ())),
                preferred_element_type=jnp.float32,
            ).astype(jnp.bfloat16)
    rows = pl.ds(pl.multiple_of(own_piece * row_count, row_count), row_count)
    new_refl, new_back, new_fore, new_under = star_rows(
        whole_ref[0, rows, :],
        whole_ref[1, rows, :],
        whole_ref[1],
        -whole_ref[0],
        whole_ref[2],
        whole_ref[3],
        whole_ref[3, rows, :],
        -whole_ref[2, rows, :],
    )
    top_ref[0] = new_under
    top_ref[1] = new_fore
    bottom_ref[0] = new_back
    bottom_ref[1] = new_refl


def level_kernel(ctl_ref, *refs):
    piece_count = (len(refs) - 6) // 2
    far_refs, low_refs = refs[:piece_count], refs[piece_count : 2 * piece_count]
    near_ref, top_ref, bottom_ref, new_top_ref, new_bottom_ref, whole_ref = refs[-6:]
    row_count = near_ref.shape[1]
    active = ctl_ref[0]
    own_piece = ctl_ref[1]

    @pl.when(active == 0)
    def _keep():
        new_top_ref[...] = top_ref[...]
        new_bottom_ref[...] = bottom_ref[...]

    for position in range(piece_count):

        @pl.when((active != 0) & (own_piece == position))
        def _place():
            for shift in range(piece_count):
                rows = slice(((position - shift) % piece_count) * row_count, None)
                rows = slice(rows.start, rows.start + row_count)
                whole_ref[0:2, rows, :] = far_refs[shift][...]
                whole_ref[2:4, rows, :] = low_refs[shift][...]

    @pl.when(active != 0)
    def _combine():
        a22 = whole_ref[0]
        a21 = whole_ref[1]
        b12 = whole_ref[2]
        b11 = whole_ref[3]
        a12 = near_ref[0]
        a11 = near_ref[1]
        b22 = top_ref[0]
        b21 = top_ref[1]
        new_refl, new_back, new_fore, new_under = star_rows(a11, a12, a21, a22, b11, b12, b21, b22)
        new_bottom_ref[1] = new_refl
        new_bottom_ref[0] = new_back
        new_top_ref[1] = new_fore
        new_top_ref[0] = new_under


def first_call(own_piece, row_count, modes_all, scales):
    ctl = own_piece.astype(jnp.int32).reshape(1)
    row_shape = jax.ShapeDtypeStruct((2, row_count, modes_all.shape[2]), modes_all.dtype)
    vmem = pl.BlockSpec(memory_space=pltpu.VMEM)
    whole_shape = (4, modes_all.shape[1], modes_all.shape[2])
    return pl.pallas_call(
        first_kernel,
        out_shape=(row_shape, row_shape),
        in_specs=[pl.BlockSpec(memory_space=pltpu.SMEM), vmem, vmem],
        out_specs=(vmem, vmem),
        scratch_shapes=[pltpu.VMEM(whole_shape, modes_all.dtype)],
    )(ctl, modes_all, scales)


def level_call(active, own_piece, far, low, near, top, bottom):
    ctl = jnp.stack([active.astype(jnp.int32), own_piece.astype(jnp.int32)])
    row_shape = jax.ShapeDtypeStruct(top.shape, top.dtype)
    whole_shape = (4, far[0].shape[1] * len(far), far[0].shape[2])
    vmem = pl.BlockSpec(memory_space=pltpu.VMEM)
    return pl.pallas_call(
        level_kernel,
        out_shape=(row_shape, row_shape),
        in_specs=[pl.BlockSpec(memory_space=pltpu.SMEM)] + [vmem] * (2 * len(far) + 3),
        out_specs=(vmem, vmem),
        scratch_shapes=[pltpu.VMEM(whole_shape, top.dtype)],
    )(ctl, *far, *low, near, top, bottom)


def spread(value, axis):
    count = lax.axis_size(axis)
    return [value] + [rotated(value, axis, shift) for shift in range(1, count)]


def on_device(mode_matrix, decay_rate, facet_refl):
    coefficients = jnp.stack([decay_rate, facet_refl], axis=-1)
    relayed_modes = lax.all_to_all(mode_matrix, "layer", split_axis=0, concat_axis=1, tiled=True)
    relayed_coeff = lax.all_to_all(coefficients, "layer", split_axis=0, concat_axis=1, tiled=True)
    relayed_decay = relayed_coeff[..., 0]
    relayed_refl = relayed_coeff[..., 1]
    block_index = lax.axis_index("blk")
    block_count = lax.axis_size("blk")
    refl_full = relayed_refl.astype(jnp.float32)
    transmit = jnp.sqrt(1.0 - refl_full * refl_full) * jnp.exp(-relayed_decay.astype(jnp.float32))
    modes_all = lax.all_gather(relayed_modes, "blk", axis=2, tiled=True)
    scales = jnp.stack([refl_full, transmit], axis=1)[:, :, None, :]
    row_count = HARM // block_count
    own_top, own_bottom = first_call(block_index, row_count, modes_all, scales)
    group_index = lax.axis_index("layer")
    level_count = lax.axis_size("layer").bit_length() - 1
    for section_level in range(level_count):
        distance = 1 << section_level
        lower_far = spread(own_bottom, "blk")
        upper_top = passed_along(own_top, "layer", distance)
        upper_top, later_bottom = lax.optimization_barrier([upper_top, own_bottom])
        upper_bottom = passed_along(later_bottom, "layer", distance)
        upper_far = spread(upper_top, "blk")
        own_top, own_bottom = level_call(
            group_index >= distance,
            block_index,
            upper_far,
            lower_far,
            upper_bottom,
            own_top,
            own_bottom,
        )
    own_rows = jnp.stack([own_bottom[1], own_bottom[0], own_top[1], own_top[0]])
    return own_rows[None]


def solution(mesh):
    placed = (P(None, "layer", "blk"), P(None, "layer"), P(None, "layer"))
    return jax.shard_map(
        on_device,
        mesh=mesh,
        in_specs=placed,
        out_specs=P("layer", None, "blk", None),
        check_vma=False,
    )
```

```python
import functools

import jax
import jax.numpy as jnp
from jax import lax
from jax.sharding import PartitionSpec as P
from jax.experimental import pallas as pl
from jax.experimental.pallas import tpu as pltpu

HARM = 512
REFL = 4


def passed_along(value, axis, steps):
    count = lax.axis_size(axis)
    first, last = (max(0, -steps), min(count, count - steps))
    return lax.ppermute(value, axis, [(source, source + steps) for source in range(first, last)])


def rotated(value, axis, steps):
    count = lax.axis_size(axis)
    return lax.ppermute(value, axis, [(source, (source + steps) % count) for source in range(count)])


def times_f32(left_op, right_op):
    return jnp.dot(left_op, right_op, preferred_element_type=jnp.float32)


def star_whole(upper_s, lower_s):
    coupling_down = times_f32(lower_s[0], upper_s[3]).astype(jnp.bfloat16)
    coupling_up = times_f32(upper_s[3], lower_s[0]).astype(jnp.bfloat16)
    left_sum = upper_s[1]
    for repeat in range(REFL):
        left_sum = (upper_s[1] + times_f32(left_sum, coupling_down)).astype(jnp.bfloat16)
    right_sum = lower_s[2]
    for repeat in range(REFL):
        right_sum = (lower_s[2] + times_f32(right_sum, coupling_up)).astype(jnp.bfloat16)
    left_mid = times_f32(left_sum, lower_s[0]).astype(jnp.bfloat16)
    right_mid = times_f32(right_sum, upper_s[3]).astype(jnp.bfloat16)
    new_refl = (upper_s[0] + times_f32(left_mid, upper_s[2])).astype(jnp.bfloat16)
    new_back = times_f32(left_sum, lower_s[1]).astype(jnp.bfloat16)
    new_fore = times_f32(right_sum, upper_s[2]).astype(jnp.bfloat16)
    new_under = (lower_s[3] + times_f32(right_mid, lower_s[1])).astype(jnp.bfloat16)
    return [new_refl, new_back, new_fore, new_under]


def assembled(pieces_ref, slot, own_piece):
    piece_count = pieces_ref.shape[0]
    return jnp.concatenate(
        [
            pieces_ref[(own_piece - source + piece_count) % piece_count, slot]
            for source in range(piece_count)
        ],
        axis=0,
    )


def star_rows(a11, a12, a21, a22, b11, b12, b21, b22):
    coupling_down = times_f32(b11, a22).astype(jnp.bfloat16)
    coupling_up = times_f32(a22, b11).astype(jnp.bfloat16)
    left_sum = a12
    for repeat in range(REFL):
        left_sum = (a12 + times_f32(left_sum, coupling_down)).astype(jnp.bfloat16)
    right_sum = b21
    for repeat in range(REFL):
        right_sum = (b21 + times_f32(right_sum, coupling_up)).astype(jnp.bfloat16)
    left_mid = times_f32(left_sum, b11).astype(jnp.bfloat16)
    right_mid = times_f32(right_sum, a22).astype(jnp.bfloat16)
    new_refl = (a11 + times_f32(left_mid, a21)).astype(jnp.bfloat16)
    new_back = times_f32(left_sum, b12).astype(jnp.bfloat16)
    new_fore = times_f32(right_sum, a21).astype(jnp.bfloat16)
    new_under = (b22 + times_f32(right_mid, b12)).astype(jnp.bfloat16)
    return new_refl, new_back, new_fore, new_under


def first_kernel(ctl_ref, modes_ref, scale_ref, top_ref, bottom_ref, whole_ref):
    own_piece = ctl_ref[0]
    row_count = top_ref.shape[1]
    for layer_pos in range(2):
        modes_one = modes_ref[layer_pos]
        modes_wide = modes_one.astype(jnp.float32)
        for kind in range(2):
            scaled = (modes_wide * scale_ref[layer_pos, kind]).astype(jnp.bfloat16)
            whole_ref[2 * layer_pos + kind] = lax.dot_general(
                modes_one,
                scaled,
                (((1,), (1,)), ((), ())),
                preferred_element_type=jnp.float32,
            ).astype(jnp.bfloat16)
    rows = pl.ds(pl.multiple_of(own_piece * row_count, row_count), row_count)
    new_refl, new_back, new_fore, new_under = star_rows(
        whole_ref[0, rows, :],
        whole_ref[1, rows, :],
        whole_ref[1],
        -whole_ref[0],
        whole_ref[2],
        whole_ref[3],
        whole_ref[3, rows, :],
        -whole_ref[2, rows, :],
    )
    top_ref[0] = new_under
    top_ref[1] = new_fore
    bottom_ref[0] = new_back
    bottom_ref[1] = new_refl


def level_kernel(ctl_ref, *refs):
    piece_count = (len(refs) - 6) // 2
    far_refs, low_refs = refs[:piece_count], refs[piece_count : 2 * piece_count]
    near_ref, top_ref, bottom_ref, new_top_ref, new_bottom_ref, whole_ref = refs[-6:]
    row_count = near_ref.shape[1]
    active = ctl_ref[0]
    own_piece = ctl_ref[1]

    @pl.when(active == 0)
    def _keep():
        new_top_ref[...] = top_ref[...]
        new_bottom_ref[...] = bottom_ref[...]

    for position in range(piece_count):

        @pl.when((active != 0) & (own_piece == position))
        def _place():
            for shift in range(piece_count):
                rows = slice(((position - shift) % piece_count) * row_count, None)
                rows = slice(rows.start, rows.start + row_count)
                whole_ref[0:2, rows, :] = far_refs[shift][...]
                whole_ref[2:4, rows, :] = low_refs[shift][...]

    @pl.when(active != 0)
    def _combine():
        a22 = whole_ref[0]
        a21 = whole_ref[1]
        b12 = whole_ref[2]
        b11 = whole_ref[3]
        a12 = near_ref[0]
        a11 = near_ref[1]
        b22 = top_ref[0]
        b21 = top_ref[1]
        new_refl, new_back, new_fore, new_under = star_rows(a11, a12, a21, a22, b11, b12, b21, b22)
        new_bottom_ref[1] = new_refl
        new_bottom_ref[0] = new_back
        new_top_ref[1] = new_fore
        new_top_ref[0] = new_under


def first_call(own_piece, row_count, modes_all, scales):
    ctl = own_piece.astype(jnp.int32).reshape(1)
    row_shape = jax.ShapeDtypeStruct((2, row_count, modes_all.shape[2]), modes_all.dtype)
    vmem = pl.BlockSpec(memory_space=pltpu.VMEM)
    whole_shape = (4, modes_all.shape[1], modes_all.shape[2])
    return pl.pallas_call(
        first_kernel,
        out_shape=(row_shape, row_shape),
        in_specs=[pl.BlockSpec(memory_space=pltpu.SMEM), vmem, vmem],
        out_specs=(vmem, vmem),
        scratch_shapes=[pltpu.VMEM(whole_shape, modes_all.dtype)],
    )(ctl, modes_all, scales)


def level_call(active, own_piece, far, low, near, top, bottom):
    ctl = jnp.stack([active.astype(jnp.int32), own_piece.astype(jnp.int32)])
    row_shape = jax.ShapeDtypeStruct(top.shape, top.dtype)
    whole_shape = (4, far[0].shape[1] * len(far), far[0].shape[2])
    vmem = pl.BlockSpec(memory_space=pltpu.VMEM)
    return pl.pallas_call(
        level_kernel,
        out_shape=(row_shape, row_shape),
        in_specs=[pl.BlockSpec(memory_space=pltpu.SMEM)] + [vmem] * (2 * len(far) + 3),
        out_specs=(vmem, vmem),
        scratch_shapes=[pltpu.VMEM(whole_shape, top.dtype)],
    )(ctl, *far, *low, near, top, bottom)


def spread(value, axis):
    count = lax.axis_size(axis)
    return [value] + [rotated(value, axis, shift) for shift in range(1, count)]


def on_device(mode_matrix, decay_rate, facet_refl):
    coefficients = jnp.stack([decay_rate, facet_refl], axis=-1)
    relayed_modes = lax.all_to_all(mode_matrix, "layer", split_axis=0, concat_axis=1, tiled=True)
    relayed_coeff = lax.all_to_all(coefficients, "layer", split_axis=0, concat_axis=1, tiled=True)
    relayed_decay = relayed_coeff[..., 0]
    relayed_refl = relayed_coeff[..., 1]
    block_index = lax.axis_index("blk")
    block_count = lax.axis_size("blk")
    refl_full = relayed_refl.astype(jnp.float32)
    transmit = jnp.sqrt(1.0 - refl_full * refl_full) * jnp.exp(-relayed_decay.astype(jnp.float32))
    modes_all = lax.all_gather(relayed_modes, "blk", axis=2, tiled=True)
    scales = jnp.stack([refl_full, transmit], axis=1)[:, :, None, :]
    row_count = HARM // block_count
    own_top, own_bottom = first_call(block_index, row_count, modes_all, scales)
    group_index = lax.axis_index("layer")
    level_count = lax.axis_size("layer").bit_length() - 1
    for section_level in range(level_count):
        distance = 1 << section_level
        lower_far = spread(own_bottom, "blk")
        upper_top = passed_along(own_top, "layer", distance)
        upper_bottom = passed_along(own_bottom, "layer", distance)
        upper_far = spread(upper_top, "blk")
        own_top, own_bottom = level_call(
            group_index >= distance,
            block_index,
            upper_far,
            lower_far,
            upper_bottom,
            own_top,
            own_bottom,
        )
    own_rows = jnp.stack([own_bottom[1], own_bottom[0], own_top[1], own_top[0]])
    return own_rows[None]


def solution(mesh):
    placed = (P(None, "layer", "blk"), P(None, "layer"), P(None, "layer"))
    return jax.shard_map(
        on_device,
        mesh=mesh,
        in_specs=placed,
        out_specs=P("layer", None, "blk", None),
        check_vma=False,
    )
```

```python
import functools

import jax
import jax.numpy as jnp
from jax import lax
from jax.sharding import PartitionSpec as P
from jax.experimental import pallas as pl
from jax.experimental.pallas import tpu as pltpu

HARM = 512
REFL = 4


def passed_along(value, axis, steps):
    count = lax.axis_size(axis)
    first, last = (max(0, -steps), min(count, count - steps))
    return lax.ppermute(value, axis, [(source, source + steps) for source in range(first, last)])


def rotated(value, axis, steps):
    count = lax.axis_size(axis)
    return lax.ppermute(value, axis, [(source, (source + steps) % count) for source in range(count)])


def times_f32(left_op, right_op):
    return jnp.dot(left_op, right_op, preferred_element_type=jnp.float32)


def star_whole(upper_s, lower_s):
    coupling_down = times_f32(lower_s[0], upper_s[3]).astype(jnp.bfloat16)
    coupling_up = times_f32(upper_s[3], lower_s[0]).astype(jnp.bfloat16)
    left_sum = upper_s[1]
    for repeat in range(REFL):
        left_sum = (upper_s[1] + times_f32(left_sum, coupling_down)).astype(jnp.bfloat16)
    right_sum = lower_s[2]
    for repeat in range(REFL):
        right_sum = (lower_s[2] + times_f32(right_sum, coupling_up)).astype(jnp.bfloat16)
    left_mid = times_f32(left_sum, lower_s[0]).astype(jnp.bfloat16)
    right_mid = times_f32(right_sum, upper_s[3]).astype(jnp.bfloat16)
    new_refl = (upper_s[0] + times_f32(left_mid, upper_s[2])).astype(jnp.bfloat16)
    new_back = times_f32(left_sum, lower_s[1]).astype(jnp.bfloat16)
    new_fore = times_f32(right_sum, upper_s[2]).astype(jnp.bfloat16)
    new_under = (lower_s[3] + times_f32(right_mid, lower_s[1])).astype(jnp.bfloat16)
    return [new_refl, new_back, new_fore, new_under]


def assembled(pieces_ref, slot, own_piece):
    piece_count = pieces_ref.shape[0]
    return jnp.concatenate(
        [
            pieces_ref[(own_piece - source + piece_count) % piece_count, slot]
            for source in range(piece_count)
        ],
        axis=0,
    )


def star_rows(a11, a12, a21, a22, b11, b12, b21, b22):
    coupling_down = times_f32(b11, a22).astype(jnp.bfloat16)
    coupling_up = times_f32(a22, b11).astype(jnp.bfloat16)
    left_sum = a12
    for repeat in range(REFL):
        left_sum = (a12 + times_f32(left_sum, coupling_down)).astype(jnp.bfloat16)
    right_sum = b21
    for repeat in range(REFL):
        right_sum = (b21 + times_f32(right_sum, coupling_up)).astype(jnp.bfloat16)
    left_mid = times_f32(left_sum, b11).astype(jnp.bfloat16)
    right_mid = times_f32(right_sum, a22).astype(jnp.bfloat16)
    new_refl = (a11 + times_f32(left_mid, a21)).astype(jnp.bfloat16)
    new_back = times_f32(left_sum, b12).astype(jnp.bfloat16)
    new_fore = times_f32(right_sum, a21).astype(jnp.bfloat16)
    new_under = (b22 + times_f32(right_mid, b12)).astype(jnp.bfloat16)
    return new_refl, new_back, new_fore, new_under


def first_kernel(ctl_ref, modes_ref, scale_ref, top_ref, bottom_ref, whole_ref):
    own_piece = ctl_ref[0]
    row_count = top_ref.shape[1]
    for layer_pos in range(2):
        modes_one = modes_ref[layer_pos]
        modes_wide = modes_one.astype(jnp.float32)
        for kind in range(2):
            scaled = (modes_wide * scale_ref[layer_pos, kind]).astype(jnp.bfloat16)
            whole_ref[2 * layer_pos + kind] = lax.dot_general(
                modes_one,
                scaled,
                (((1,), (1,)), ((), ())),
                preferred_element_type=jnp.float32,
            ).astype(jnp.bfloat16)
    rows = pl.ds(pl.multiple_of(own_piece * row_count, row_count), row_count)
    new_refl, new_back, new_fore, new_under = star_rows(
        whole_ref[0, rows, :],
        whole_ref[1, rows, :],
        whole_ref[1],
        -whole_ref[0],
        whole_ref[2],
        whole_ref[3],
        whole_ref[3, rows, :],
        -whole_ref[2, rows, :],
    )
    top_ref[0] = new_under
    top_ref[1] = new_fore
    bottom_ref[0] = new_back
    bottom_ref[1] = new_refl


def level_kernel(ctl_ref, *refs):
    piece_count = len(refs) - 7
    far_refs, low_ref = refs[:piece_count], refs[piece_count]
    near_ref, top_ref, bottom_ref, new_top_ref, new_bottom_ref, whole_ref = refs[-6:]
    row_count = near_ref.shape[1]
    active = ctl_ref[0]
    own_piece = ctl_ref[1]

    @pl.when(active == 0)
    def _keep():
        new_top_ref[...] = top_ref[...]
        new_bottom_ref[...] = bottom_ref[...]

    for position in range(piece_count):

        @pl.when((active != 0) & (own_piece == position))
        def _place():
            for shift in range(piece_count):
                rows = slice(((position - shift) % piece_count) * row_count, None)
                rows = slice(rows.start, rows.start + row_count)
                whole_ref[0:2, rows, :] = far_refs[shift][...]

    @pl.when(active != 0)
    def _combine():
        for source in range(piece_count):
            whole_ref[2:4, source * row_count : (source + 1) * row_count, :] = low_ref[source]
        a22 = whole_ref[0]
        a21 = whole_ref[1]
        b12 = whole_ref[2]
        b11 = whole_ref[3]
        a12 = near_ref[0]
        a11 = near_ref[1]
        b22 = top_ref[0]
        b21 = top_ref[1]
        new_refl, new_back, new_fore, new_under = star_rows(a11, a12, a21, a22, b11, b12, b21, b22)
        new_bottom_ref[1] = new_refl
        new_bottom_ref[0] = new_back
        new_top_ref[1] = new_fore
        new_top_ref[0] = new_under


def first_call(own_piece, row_count, modes_all, scales):
    ctl = own_piece.astype(jnp.int32).reshape(1)
    row_shape = jax.ShapeDtypeStruct((2, row_count, modes_all.shape[2]), modes_all.dtype)
    vmem = pl.BlockSpec(memory_space=pltpu.VMEM)
    whole_shape = (4, modes_all.shape[1], modes_all.shape[2])
    return pl.pallas_call(
        first_kernel,
        out_shape=(row_shape, row_shape),
        in_specs=[pl.BlockSpec(memory_space=pltpu.SMEM), vmem, vmem],
        out_specs=(vmem, vmem),
        scratch_shapes=[pltpu.VMEM(whole_shape, modes_all.dtype)],
    )(ctl, modes_all, scales)


def level_call(active, own_piece, far, low, near, top, bottom):
    ctl = jnp.stack([active.astype(jnp.int32), own_piece.astype(jnp.int32)])
    row_shape = jax.ShapeDtypeStruct(top.shape, top.dtype)
    whole_shape = (4, far[0].shape[1] * len(far), far[0].shape[2])
    vmem = pl.BlockSpec(memory_space=pltpu.VMEM)
    return pl.pallas_call(
        level_kernel,
        out_shape=(row_shape, row_shape),
        in_specs=[pl.BlockSpec(memory_space=pltpu.SMEM)] + [vmem] * (len(far) + 4),
        out_specs=(vmem, vmem),
        scratch_shapes=[pltpu.VMEM(whole_shape, top.dtype)],
    )(ctl, *far, low, near, top, bottom)


def spread(value, axis):
    count = lax.axis_size(axis)
    return [value] + [rotated(value, axis, shift) for shift in range(1, count)]


def on_device(mode_matrix, decay_rate, facet_refl):
    coefficients = jnp.stack([decay_rate, facet_refl], axis=-1)
    relayed_modes = lax.all_to_all(mode_matrix, "layer", split_axis=0, concat_axis=1, tiled=True)
    relayed_coeff = lax.all_to_all(coefficients, "layer", split_axis=0, concat_axis=1, tiled=True)
    relayed_decay = relayed_coeff[..., 0]
    relayed_refl = relayed_coeff[..., 1]
    block_index = lax.axis_index("blk")
    block_count = lax.axis_size("blk")
    refl_full = relayed_refl.astype(jnp.float32)
    transmit = jnp.sqrt(1.0 - refl_full * refl_full) * jnp.exp(-relayed_decay.astype(jnp.float32))
    modes_all = lax.all_gather(relayed_modes, "blk", axis=2, tiled=True)
    scales = jnp.stack([refl_full, transmit], axis=1)[:, :, None, :]
    row_count = HARM // block_count
    own_top, own_bottom = first_call(block_index, row_count, modes_all, scales)
    group_index = lax.axis_index("layer")
    level_count = lax.axis_size("layer").bit_length() - 1
    for section_level in range(level_count):
        distance = 1 << section_level
        lower_far = lax.all_gather(own_bottom, "blk", axis=0, tiled=False)
        upper_top = passed_along(own_top, "layer", distance)
        upper_bottom = passed_along(own_bottom, "layer", distance)
        upper_far = spread(upper_top, "blk")
        own_top, own_bottom = level_call(
            group_index >= distance,
            block_index,
            upper_far,
            lower_far,
            upper_bottom,
            own_top,
            own_bottom,
        )
    own_rows = jnp.stack([own_bottom[1], own_bottom[0], own_top[1], own_top[0]])
    return own_rows[None]


def solution(mesh):
    placed = (P(None, "layer", "blk"), P(None, "layer"), P(None, "layer"))
    return jax.shard_map(
        on_device,
        mesh=mesh,
        in_specs=placed,
        out_specs=P("layer", None, "blk", None),
        check_vma=False,
    )
```

```python
import functools

import jax
import jax.numpy as jnp
from jax import lax
from jax.sharding import PartitionSpec as P
from jax.experimental import pallas as pl
from jax.experimental.pallas import tpu as pltpu

HARM = 512
REFL = 4


def passed_along(value, axis, steps):
    count = lax.axis_size(axis)
    first, last = (max(0, -steps), min(count, count - steps))
    return lax.ppermute(value, axis, [(source, source + steps) for source in range(first, last)])


def rotated(value, axis, steps):
    count = lax.axis_size(axis)
    return lax.ppermute(value, axis, [(source, (source + steps) % count) for source in range(count)])


def times_f32(left_op, right_op):
    return jnp.dot(left_op, right_op, preferred_element_type=jnp.float32)


def star_whole(upper_s, lower_s):
    coupling_down = times_f32(lower_s[0], upper_s[3]).astype(jnp.bfloat16)
    coupling_up = times_f32(upper_s[3], lower_s[0]).astype(jnp.bfloat16)
    left_sum = upper_s[1]
    for repeat in range(REFL):
        left_sum = (upper_s[1] + times_f32(left_sum, coupling_down)).astype(jnp.bfloat16)
    right_sum = lower_s[2]
    for repeat in range(REFL):
        right_sum = (lower_s[2] + times_f32(right_sum, coupling_up)).astype(jnp.bfloat16)
    left_mid = times_f32(left_sum, lower_s[0]).astype(jnp.bfloat16)
    right_mid = times_f32(right_sum, upper_s[3]).astype(jnp.bfloat16)
    new_refl = (upper_s[0] + times_f32(left_mid, upper_s[2])).astype(jnp.bfloat16)
    new_back = times_f32(left_sum, lower_s[1]).astype(jnp.bfloat16)
    new_fore = times_f32(right_sum, upper_s[2]).astype(jnp.bfloat16)
    new_under = (lower_s[3] + times_f32(right_mid, lower_s[1])).astype(jnp.bfloat16)
    return [new_refl, new_back, new_fore, new_under]


def assembled(pieces_ref, slot, own_piece):
    piece_count = pieces_ref.shape[0]
    return jnp.concatenate(
        [
            pieces_ref[(own_piece - source + piece_count) % piece_count, slot]
            for source in range(piece_count)
        ],
        axis=0,
    )


def star_rows(a11, a12, a21, a22, b11, b12, b21, b22):
    coupling_down = times_f32(b11, a22).astype(jnp.bfloat16)
    coupling_up = times_f32(a22, b11).astype(jnp.bfloat16)
    left_sum = a12
    for repeat in range(REFL):
        left_sum = (a12 + times_f32(left_sum, coupling_down)).astype(jnp.bfloat16)
    right_sum = b21
    for repeat in range(REFL):
        right_sum = (b21 + times_f32(right_sum, coupling_up)).astype(jnp.bfloat16)
    left_mid = times_f32(left_sum, b11).astype(jnp.bfloat16)
    right_mid = times_f32(right_sum, a22).astype(jnp.bfloat16)
    new_refl = (a11 + times_f32(left_mid, a21)).astype(jnp.bfloat16)
    new_back = times_f32(left_sum, b12).astype(jnp.bfloat16)
    new_fore = times_f32(right_sum, a21).astype(jnp.bfloat16)
    new_under = (b22 + times_f32(right_mid, b12)).astype(jnp.bfloat16)
    return new_refl, new_back, new_fore, new_under


def first_kernel(ctl_ref, modes_ref, scale_ref, top_ref, bottom_ref, whole_ref):
    own_piece = ctl_ref[0]
    row_count = top_ref.shape[1]
    for layer_pos in range(2):
        modes_one = modes_ref[layer_pos]
        modes_wide = modes_one.astype(jnp.float32)
        for kind in range(2):
            scaled = (modes_wide * scale_ref[layer_pos, kind]).astype(jnp.bfloat16)
            whole_ref[2 * layer_pos + kind] = lax.dot_general(
                modes_one,
                scaled,
                (((1,), (1,)), ((), ())),
                preferred_element_type=jnp.float32,
            ).astype(jnp.bfloat16)
    rows = pl.ds(pl.multiple_of(own_piece * row_count, row_count), row_count)
    new_refl, new_back, new_fore, new_under = star_rows(
        whole_ref[0, rows, :],
        whole_ref[1, rows, :],
        whole_ref[1],
        -whole_ref[0],
        whole_ref[2],
        whole_ref[3],
        whole_ref[3, rows, :],
        -whole_ref[2, rows, :],
    )
    top_ref[0] = new_under
    top_ref[1] = new_fore
    bottom_ref[0] = new_back
    bottom_ref[1] = new_refl


def level_kernel(ctl_ref, *refs):
    piece_count = (len(refs) - 6) // 2
    far_refs, low_refs = refs[:piece_count], refs[piece_count : 2 * piece_count]
    near_ref, top_ref, bottom_ref, new_top_ref, new_bottom_ref, whole_ref = refs[-6:]
    row_count = near_ref.shape[1]
    active = ctl_ref[0]
    own_piece = ctl_ref[1]

    @pl.when(active == 0)
    def _keep():
        new_top_ref[...] = top_ref[...]
        new_bottom_ref[...] = bottom_ref[...]

    for position in range(piece_count):

        @pl.when((active != 0) & (own_piece == position))
        def _place():
            for shift in range(piece_count):
                rows = slice(((position - shift) % piece_count) * row_count, None)
                rows = slice(rows.start, rows.start + row_count)
                whole_ref[0:2, rows, :] = far_refs[shift][...]
                whole_ref[2:4, rows, :] = low_refs[shift][...]

    @pl.when(active != 0)
    def _combine():
        a22 = whole_ref[0]
        a21 = whole_ref[1]
        b12 = whole_ref[2]
        b11 = whole_ref[3]
        a12 = near_ref[0]
        a11 = near_ref[1]
        b22 = top_ref[0]
        b21 = top_ref[1]
        new_refl, new_back, new_fore, new_under = star_rows(a11, a12, a21, a22, b11, b12, b21, b22)
        new_bottom_ref[1] = new_refl
        new_bottom_ref[0] = new_back
        new_top_ref[1] = new_fore
        new_top_ref[0] = new_under


def first_call(own_piece, row_count, modes_all, scales):
    ctl = own_piece.astype(jnp.int32).reshape(1)
    row_shape = jax.ShapeDtypeStruct((2, row_count, modes_all.shape[2]), modes_all.dtype)
    vmem = pl.BlockSpec(memory_space=pltpu.VMEM)
    whole_shape = (4, modes_all.shape[1], modes_all.shape[2])
    return pl.pallas_call(
        first_kernel,
        out_shape=(row_shape, row_shape),
        in_specs=[pl.BlockSpec(memory_space=pltpu.SMEM), vmem, vmem],
        out_specs=(vmem, vmem),
        scratch_shapes=[pltpu.VMEM(whole_shape, modes_all.dtype)],
    )(ctl, modes_all, scales)


def level_call(active, own_piece, far, low, near, top, bottom):
    ctl = jnp.stack([active.astype(jnp.int32), own_piece.astype(jnp.int32)])
    row_shape = jax.ShapeDtypeStruct(top.shape, top.dtype)
    whole_shape = (4, far[0].shape[1] * len(far), far[0].shape[2])
    vmem = pl.BlockSpec(memory_space=pltpu.VMEM)
    return pl.pallas_call(
        level_kernel,
        out_shape=(row_shape, row_shape),
        in_specs=[pl.BlockSpec(memory_space=pltpu.SMEM)] + [vmem] * (2 * len(far) + 3),
        out_specs=(vmem, vmem),
        scratch_shapes=[pltpu.VMEM(whole_shape, top.dtype)],
    )(ctl, *far, *low, near, top, bottom)


def spread(value, axis):
    count = lax.axis_size(axis)
    return [value] + [rotated(value, axis, shift) for shift in range(1, count)]


def on_device(mode_matrix, decay_rate, facet_refl):
    coefficients = jnp.stack([decay_rate, facet_refl], axis=-1)
    relayed_modes = lax.all_to_all(mode_matrix, "layer", split_axis=0, concat_axis=1, tiled=True)
    relayed_coeff = lax.all_to_all(coefficients, "layer", split_axis=0, concat_axis=1, tiled=True)
    relayed_decay = relayed_coeff[..., 0]
    relayed_refl = relayed_coeff[..., 1]
    block_index = lax.axis_index("blk")
    block_count = lax.axis_size("blk")
    refl_full = relayed_refl.astype(jnp.float32)
    transmit = jnp.sqrt(1.0 - refl_full * refl_full) * jnp.exp(-relayed_decay.astype(jnp.float32))
    modes_all = lax.all_gather(relayed_modes, "blk", axis=2, tiled=True)
    scales = jnp.stack([refl_full, transmit], axis=1)[:, :, None, :]
    row_count = HARM // block_count
    own_top, own_bottom = first_call(block_index, row_count, modes_all, scales)
    group_index = lax.axis_index("layer")
    level_count = lax.axis_size("layer").bit_length() - 1
    for section_level in range(level_count):
        distance = 1 << section_level
        upper_top = passed_along(own_top, "layer", distance)
        upper_bottom = passed_along(own_bottom, "layer", distance)
        upper_top, later_bottom = lax.optimization_barrier([upper_top, own_bottom])
        upper_far = spread(upper_top, "blk")
        lower_far = spread(later_bottom, "blk")
        own_top, own_bottom = level_call(
            group_index >= distance,
            block_index,
            upper_far,
            lower_far,
            upper_bottom,
            own_top,
            own_bottom,
        )
    own_rows = jnp.stack([own_bottom[1], own_bottom[0], own_top[1], own_top[0]])
    return own_rows[None]


def solution(mesh):
    placed = (P(None, "layer", "blk"), P(None, "layer"), P(None, "layer"))
    return jax.shard_map(
        on_device,
        mesh=mesh,
        in_specs=placed,
        out_specs=P("layer", None, "blk", None),
        check_vma=False,
    )
```

```python
import functools

import jax
import jax.numpy as jnp
from jax import lax
from jax.sharding import PartitionSpec as P
from jax.experimental import pallas as pl
from jax.experimental.pallas import tpu as pltpu

HARM = 512
REFL = 4


def passed_along(value, axis, steps):
    count = lax.axis_size(axis)
    first, last = (max(0, -steps), min(count, count - steps))
    return lax.ppermute(value, axis, [(source, source + steps) for source in range(first, last)])


def rotated(value, axis, steps):
    count = lax.axis_size(axis)
    return lax.ppermute(value, axis, [(source, (source + steps) % count) for source in range(count)])


def times_f32(left_op, right_op):
    return jnp.dot(left_op, right_op, preferred_element_type=jnp.float32)


def star_whole(upper_s, lower_s):
    coupling_down = times_f32(lower_s[0], upper_s[3]).astype(jnp.bfloat16)
    coupling_up = times_f32(upper_s[3], lower_s[0]).astype(jnp.bfloat16)
    left_sum = upper_s[1]
    for repeat in range(REFL):
        left_sum = (upper_s[1] + times_f32(left_sum, coupling_down)).astype(jnp.bfloat16)
    right_sum = lower_s[2]
    for repeat in range(REFL):
        right_sum = (lower_s[2] + times_f32(right_sum, coupling_up)).astype(jnp.bfloat16)
    left_mid = times_f32(left_sum, lower_s[0]).astype(jnp.bfloat16)
    right_mid = times_f32(right_sum, upper_s[3]).astype(jnp.bfloat16)
    new_refl = (upper_s[0] + times_f32(left_mid, upper_s[2])).astype(jnp.bfloat16)
    new_back = times_f32(left_sum, lower_s[1]).astype(jnp.bfloat16)
    new_fore = times_f32(right_sum, upper_s[2]).astype(jnp.bfloat16)
    new_under = (lower_s[3] + times_f32(right_mid, lower_s[1])).astype(jnp.bfloat16)
    return [new_refl, new_back, new_fore, new_under]


def assembled(pieces_ref, slot, own_piece):
    piece_count = pieces_ref.shape[0]
    return jnp.concatenate(
        [
            pieces_ref[(own_piece - source + piece_count) % piece_count, slot]
            for source in range(piece_count)
        ],
        axis=0,
    )


def star_rows(a11, a12, a21, a22, b11, b12, b21, b22):
    coupling_down = times_f32(b11, a22).astype(jnp.bfloat16)
    coupling_up = times_f32(a22, b11).astype(jnp.bfloat16)
    left_sum = a12
    for repeat in range(REFL):
        left_sum = (a12 + times_f32(left_sum, coupling_down)).astype(jnp.bfloat16)
    right_sum = b21
    for repeat in range(REFL):
        right_sum = (b21 + times_f32(right_sum, coupling_up)).astype(jnp.bfloat16)
    left_mid = times_f32(left_sum, b11).astype(jnp.bfloat16)
    right_mid = times_f32(right_sum, a22).astype(jnp.bfloat16)
    new_refl = (a11 + times_f32(left_mid, a21)).astype(jnp.bfloat16)
    new_back = times_f32(left_sum, b12).astype(jnp.bfloat16)
    new_fore = times_f32(right_sum, a21).astype(jnp.bfloat16)
    new_under = (b22 + times_f32(right_mid, b12)).astype(jnp.bfloat16)
    return new_refl, new_back, new_fore, new_under


def first_kernel(ctl_ref, modes_ref, scale_ref, top_ref, bottom_ref, whole_ref):
    own_piece = ctl_ref[0]
    row_count = top_ref.shape[1]
    for layer_pos in range(2):
        modes_one = modes_ref[layer_pos]
        modes_wide = modes_one.astype(jnp.float32)
        for kind in range(2):
            scaled = (modes_wide * scale_ref[layer_pos, kind]).astype(jnp.bfloat16)
            whole_ref[2 * layer_pos + kind] = lax.dot_general(
                modes_one,
                scaled,
                (((1,), (1,)), ((), ())),
                preferred_element_type=jnp.float32,
            ).astype(jnp.bfloat16)
    rows = pl.ds(pl.multiple_of(own_piece * row_count, row_count), row_count)
    new_refl, new_back, new_fore, new_under = star_rows(
        whole_ref[0, rows, :],
        whole_ref[1, rows, :],
        whole_ref[1],
        -whole_ref[0],
        whole_ref[2],
        whole_ref[3],
        whole_ref[3, rows, :],
        -whole_ref[2, rows, :],
    )
    top_ref[0] = new_under
    top_ref[1] = new_fore
    bottom_ref[0] = new_back
    bottom_ref[1] = new_refl


def level_kernel(ctl_ref, *refs):
    piece_count = (len(refs) - 6) // 2
    far_refs, low_refs = refs[:piece_count], refs[piece_count : 2 * piece_count]
    near_ref, top_ref, bottom_ref, new_top_ref, new_bottom_ref, whole_ref = refs[-6:]
    row_count = near_ref.shape[1]
    active = ctl_ref[0]
    own_piece = ctl_ref[1]

    @pl.when(active == 0)
    def _keep():
        new_top_ref[...] = top_ref[...]
        new_bottom_ref[...] = bottom_ref[...]

    @pl.when(active != 0)
    def _place():
        for shift in range(piece_count):
            source = (own_piece - shift + piece_count) % piece_count
            rows = pl.ds(pl.multiple_of(source * row_count, row_count), row_count)
            whole_ref[0:2, rows, :] = far_refs[shift][...]
            whole_ref[2:4, rows, :] = low_refs[shift][...]

    @pl.when(active != 0)
    def _combine():
        a22 = whole_ref[0]
        a21 = whole_ref[1]
        b12 = whole_ref[2]
        b11 = whole_ref[3]
        a12 = near_ref[0]
        a11 = near_ref[1]
        b22 = top_ref[0]
        b21 = top_ref[1]
        new_refl, new_back, new_fore, new_under = star_rows(a11, a12, a21, a22, b11, b12, b21, b22)
        new_bottom_ref[1] = new_refl
        new_bottom_ref[0] = new_back
        new_top_ref[1] = new_fore
        new_top_ref[0] = new_under


def first_call(own_piece, row_count, modes_all, scales):
    ctl = own_piece.astype(jnp.int32).reshape(1)
    row_shape = jax.ShapeDtypeStruct((2, row_count, modes_all.shape[2]), modes_all.dtype)
    vmem = pl.BlockSpec(memory_space=pltpu.VMEM)
    whole_shape = (4, modes_all.shape[1], modes_all.shape[2])
    return pl.pallas_call(
        first_kernel,
        out_shape=(row_shape, row_shape),
        in_specs=[pl.BlockSpec(memory_space=pltpu.SMEM), vmem, vmem],
        out_specs=(vmem, vmem),
        scratch_shapes=[pltpu.VMEM(whole_shape, modes_all.dtype)],
    )(ctl, modes_all, scales)


def level_call(active, own_piece, far, low, near, top, bottom):
    ctl = jnp.stack([active.astype(jnp.int32), own_piece.astype(jnp.int32)])
    row_shape = jax.ShapeDtypeStruct(top.shape, top.dtype)
    whole_shape = (4, far[0].shape[1] * len(far), far[0].shape[2])
    vmem = pl.BlockSpec(memory_space=pltpu.VMEM)
    return pl.pallas_call(
        level_kernel,
        out_shape=(row_shape, row_shape),
        in_specs=[pl.BlockSpec(memory_space=pltpu.SMEM)] + [vmem] * (2 * len(far) + 3),
        out_specs=(vmem, vmem),
        scratch_shapes=[pltpu.VMEM(whole_shape, top.dtype)],
    )(ctl, *far, *low, near, top, bottom)


def spread(value, axis):
    count = lax.axis_size(axis)
    return [value] + [rotated(value, axis, shift) for shift in range(1, count)]


def on_device(mode_matrix, decay_rate, facet_refl):
    coefficients = jnp.stack([decay_rate, facet_refl], axis=-1)
    relayed_modes = lax.all_to_all(mode_matrix, "layer", split_axis=0, concat_axis=1, tiled=True)
    relayed_coeff = lax.all_to_all(coefficients, "layer", split_axis=0, concat_axis=1, tiled=True)
    relayed_decay = relayed_coeff[..., 0]
    relayed_refl = relayed_coeff[..., 1]
    block_index = lax.axis_index("blk")
    block_count = lax.axis_size("blk")
    refl_full = relayed_refl.astype(jnp.float32)
    transmit = jnp.sqrt(1.0 - refl_full * refl_full) * jnp.exp(-relayed_decay.astype(jnp.float32))
    modes_all = lax.all_gather(relayed_modes, "blk", axis=2, tiled=True)
    scales = jnp.stack([refl_full, transmit], axis=1)[:, :, None, :]
    row_count = HARM // block_count
    own_top, own_bottom = first_call(block_index, row_count, modes_all, scales)
    group_index = lax.axis_index("layer")
    level_count = lax.axis_size("layer").bit_length() - 1
    for section_level in range(level_count):
        distance = 1 << section_level
        lower_far = spread(own_bottom, "blk")
        upper_top = passed_along(own_top, "layer", distance)
        upper_bottom = passed_along(own_bottom, "layer", distance)
        upper_far = spread(upper_top, "blk")
        own_top, own_bottom = level_call(
            group_index >= distance,
            block_index,
            upper_far,
            lower_far,
            upper_bottom,
            own_top,
            own_bottom,
        )
    own_rows = jnp.stack([own_bottom[1], own_bottom[0], own_top[1], own_top[0]])
    return own_rows[None]


def solution(mesh):
    placed = (P(None, "layer", "blk"), P(None, "layer"), P(None, "layer"))
    return jax.shard_map(
        on_device,
        mesh=mesh,
        in_specs=placed,
        out_specs=P("layer", None, "blk", None),
        check_vma=False,
    )
```

```python
import functools

import jax
import jax.numpy as jnp
from jax import lax
from jax.sharding import PartitionSpec as P
from jax.experimental import pallas as pl
from jax.experimental.pallas import tpu as pltpu

HARM = 512
REFL = 4


def passed_along(value, axis, steps):
    count = lax.axis_size(axis)
    first, last = (max(0, -steps), min(count, count - steps))
    return lax.ppermute(value, axis, [(source, source + steps) for source in range(first, last)])


def rotated(value, axis, steps):
    count = lax.axis_size(axis)
    return lax.ppermute(value, axis, [(source, (source + steps) % count) for source in range(count)])


def times_f32(left_op, right_op):
    return jnp.dot(left_op, right_op, preferred_element_type=jnp.float32)


def star_whole(upper_s, lower_s):
    coupling_down = times_f32(lower_s[0], upper_s[3]).astype(jnp.bfloat16)
    coupling_up = times_f32(upper_s[3], lower_s[0]).astype(jnp.bfloat16)
    left_sum = upper_s[1]
    for repeat in range(REFL):
        left_sum = (upper_s[1] + times_f32(left_sum, coupling_down)).astype(jnp.bfloat16)
    right_sum = lower_s[2]
    for repeat in range(REFL):
        right_sum = (lower_s[2] + times_f32(right_sum, coupling_up)).astype(jnp.bfloat16)
    left_mid = times_f32(left_sum, lower_s[0]).astype(jnp.bfloat16)
    right_mid = times_f32(right_sum, upper_s[3]).astype(jnp.bfloat16)
    new_refl = (upper_s[0] + times_f32(left_mid, upper_s[2])).astype(jnp.bfloat16)
    new_back = times_f32(left_sum, lower_s[1]).astype(jnp.bfloat16)
    new_fore = times_f32(right_sum, upper_s[2]).astype(jnp.bfloat16)
    new_under = (lower_s[3] + times_f32(right_mid, lower_s[1])).astype(jnp.bfloat16)
    return [new_refl, new_back, new_fore, new_under]


def assembled(pieces_ref, slot, own_piece):
    piece_count = pieces_ref.shape[0]
    return jnp.concatenate(
        [
            pieces_ref[(own_piece - source + piece_count) % piece_count, slot]
            for source in range(piece_count)
        ],
        axis=0,
    )


def star_rows(a11, a12, a21, a22, b11, b12, b21, b22):
    coupling_down = times_f32(b11, a22).astype(jnp.bfloat16)
    coupling_up = times_f32(a22, b11).astype(jnp.bfloat16)
    left_sum = a12
    for repeat in range(REFL):
        left_sum = (a12 + times_f32(left_sum, coupling_down)).astype(jnp.bfloat16)
    right_sum = b21
    for repeat in range(REFL):
        right_sum = (b21 + times_f32(right_sum, coupling_up)).astype(jnp.bfloat16)
    left_mid = times_f32(left_sum, b11).astype(jnp.bfloat16)
    right_mid = times_f32(right_sum, a22).astype(jnp.bfloat16)
    new_refl = (a11 + times_f32(left_mid, a21)).astype(jnp.bfloat16)
    new_back = times_f32(left_sum, b12).astype(jnp.bfloat16)
    new_fore = times_f32(right_sum, a21).astype(jnp.bfloat16)
    new_under = (b22 + times_f32(right_mid, b12)).astype(jnp.bfloat16)
    return new_refl, new_back, new_fore, new_under


def first_kernel(ctl_ref, modes_ref, scale_ref, top_ref, bottom_ref, rows_ref, whole_ref):
    own_piece = ctl_ref[0]
    row_count = top_ref.shape[1]
    for layer_pos in range(2):
        modes_one = modes_ref[layer_pos]
        modes_wide = modes_one.astype(jnp.float32)
        for kind in range(2):
            scaled = (modes_wide * scale_ref[layer_pos, kind]).astype(jnp.bfloat16)
            whole_ref[2 * layer_pos + kind] = lax.dot_general(
                modes_one,
                scaled,
                (((1,), (1,)), ((), ())),
                preferred_element_type=jnp.float32,
            ).astype(jnp.bfloat16)
    rows = pl.ds(pl.multiple_of(own_piece * row_count, row_count), row_count)
    new_refl, new_back, new_fore, new_under = star_rows(
        whole_ref[0, rows, :],
        whole_ref[1, rows, :],
        whole_ref[1],
        -whole_ref[0],
        whole_ref[2],
        whole_ref[3],
        whole_ref[3, rows, :],
        -whole_ref[2, rows, :],
    )
    top_ref[0] = new_under
    top_ref[1] = new_fore
    bottom_ref[0] = new_back
    bottom_ref[1] = new_refl
    rows_ref[0:2] = top_ref[...]
    rows_ref[2:4] = bottom_ref[...]


def level_kernel(ctl_ref, *refs):
    piece_count = (len(refs) - 7) // 2
    far_refs, low_refs = refs[:piece_count], refs[piece_count : 2 * piece_count]
    near_ref, top_ref, bottom_ref, new_top_ref, new_bottom_ref, new_rows_ref, whole_ref = refs[-7:]
    row_count = near_ref.shape[1]
    active = ctl_ref[0]
    own_piece = ctl_ref[1]

    @pl.when(active == 0)
    def _keep():
        new_top_ref[...] = top_ref[...]
        new_bottom_ref[...] = bottom_ref[...]

    @pl.when(active != 0)
    def _place():
        for shift in range(piece_count):
            source = (own_piece - shift + piece_count) % piece_count
            rows = pl.ds(pl.multiple_of(source * row_count, row_count), row_count)
            whole_ref[0:2, rows, :] = far_refs[shift][...]
            whole_ref[2:4, rows, :] = low_refs[shift][...]

    @pl.when(active != 0)
    def _combine():
        a22 = whole_ref[0]
        a21 = whole_ref[1]
        b12 = whole_ref[2]
        b11 = whole_ref[3]
        a12 = near_ref[2]
        a11 = near_ref[3]
        b22 = top_ref[0]
        b21 = top_ref[1]
        new_refl, new_back, new_fore, new_under = star_rows(a11, a12, a21, a22, b11, b12, b21, b22)
        new_bottom_ref[1] = new_refl
        new_bottom_ref[0] = new_back
        new_top_ref[1] = new_fore
        new_top_ref[0] = new_under

    new_rows_ref[0:2] = new_top_ref[...]
    new_rows_ref[2:4] = new_bottom_ref[...]


def first_call(own_piece, row_count, modes_all, scales):
    ctl = own_piece.astype(jnp.int32).reshape(1)
    row_shape = jax.ShapeDtypeStruct((2, row_count, modes_all.shape[2]), modes_all.dtype)
    both_shape = jax.ShapeDtypeStruct((4, row_count, modes_all.shape[2]), modes_all.dtype)
    vmem = pl.BlockSpec(memory_space=pltpu.VMEM)
    whole_shape = (4, modes_all.shape[1], modes_all.shape[2])
    return pl.pallas_call(
        first_kernel,
        out_shape=(row_shape, row_shape, both_shape),
        in_specs=[pl.BlockSpec(memory_space=pltpu.SMEM), vmem, vmem],
        out_specs=(vmem, vmem, vmem),
        scratch_shapes=[pltpu.VMEM(whole_shape, modes_all.dtype)],
    )(ctl, modes_all, scales)


def level_call(active, own_piece, far, low, near, top, bottom):
    ctl = jnp.stack([active.astype(jnp.int32), own_piece.astype(jnp.int32)])
    row_shape = jax.ShapeDtypeStruct(top.shape, top.dtype)
    both_shape = jax.ShapeDtypeStruct((4,) + top.shape[1:], top.dtype)
    whole_shape = (4, far[0].shape[1] * len(far), far[0].shape[2])
    vmem = pl.BlockSpec(memory_space=pltpu.VMEM)
    return pl.pallas_call(
        level_kernel,
        out_shape=(row_shape, row_shape, both_shape),
        in_specs=[pl.BlockSpec(memory_space=pltpu.SMEM)] + [vmem] * (2 * len(far) + 3),
        out_specs=(vmem, vmem, vmem),
        scratch_shapes=[pltpu.VMEM(whole_shape, top.dtype)],
    )(ctl, *far, *low, near, top, bottom)


def spread(value, axis):
    count = lax.axis_size(axis)
    return [value] + [rotated(value, axis, shift) for shift in range(1, count)]


def on_device(mode_matrix, decay_rate, facet_refl):
    coefficients = jnp.stack([decay_rate, facet_refl], axis=-1)
    relayed_modes = lax.all_to_all(mode_matrix, "layer", split_axis=0, concat_axis=1, tiled=True)
    relayed_coeff = lax.all_to_all(coefficients, "layer", split_axis=0, concat_axis=1, tiled=True)
    relayed_decay = relayed_coeff[..., 0]
    relayed_refl = relayed_coeff[..., 1]
    block_index = lax.axis_index("blk")
    block_count = lax.axis_size("blk")
    refl_full = relayed_refl.astype(jnp.float32)
    transmit = jnp.sqrt(1.0 - refl_full * refl_full) * jnp.exp(-relayed_decay.astype(jnp.float32))
    modes_all = lax.all_gather(relayed_modes, "blk", axis=2, tiled=True)
    scales = jnp.stack([refl_full, transmit], axis=1)[:, :, None, :]
    row_count = HARM // block_count
    own_top, own_bottom, own_rows = first_call(block_index, row_count, modes_all, scales)
    group_index = lax.axis_index("layer")
    level_count = lax.axis_size("layer").bit_length() - 1
    for section_level in range(level_count):
        distance = 1 << section_level
        lower_far = spread(own_bottom, "blk")
        upper_rows = passed_along(own_rows, "layer", distance)
        upper_far = spread(upper_rows[0:2], "blk")
        own_top, own_bottom, own_rows = level_call(
            group_index >= distance,
            block_index,
            upper_far,
            lower_far,
            upper_rows,
            own_top,
            own_bottom,
        )
    own_rows = jnp.stack([own_bottom[1], own_bottom[0], own_top[1], own_top[0]])
    return own_rows[None]


def solution(mesh):
    placed = (P(None, "layer", "blk"), P(None, "layer"), P(None, "layer"))
    return jax.shard_map(
        on_device,
        mesh=mesh,
        in_specs=placed,
        out_specs=P("layer", None, "blk", None),
        check_vma=False,
    )
```

```python
import functools

import jax
import jax.numpy as jnp
from jax import lax
from jax.sharding import PartitionSpec as P
from jax.experimental import pallas as pl
from jax.experimental.pallas import tpu as pltpu

HARM = 512
REFL = 4


def passed_along(value, axis, steps):
    count = lax.axis_size(axis)
    first, last = (max(0, -steps), min(count, count - steps))
    return lax.ppermute(value, axis, [(source, source + steps) for source in range(first, last)])


def rotated(value, axis, steps):
    count = lax.axis_size(axis)
    return lax.ppermute(value, axis, [(source, (source + steps) % count) for source in range(count)])


def times_f32(left_op, right_op):
    return jnp.dot(left_op, right_op, preferred_element_type=jnp.float32)


def star_whole(upper_s, lower_s):
    coupling_down = times_f32(lower_s[0], upper_s[3]).astype(jnp.bfloat16)
    coupling_up = times_f32(upper_s[3], lower_s[0]).astype(jnp.bfloat16)
    left_sum = upper_s[1]
    for repeat in range(REFL):
        left_sum = (upper_s[1] + times_f32(left_sum, coupling_down)).astype(jnp.bfloat16)
    right_sum = lower_s[2]
    for repeat in range(REFL):
        right_sum = (lower_s[2] + times_f32(right_sum, coupling_up)).astype(jnp.bfloat16)
    left_mid = times_f32(left_sum, lower_s[0]).astype(jnp.bfloat16)
    right_mid = times_f32(right_sum, upper_s[3]).astype(jnp.bfloat16)
    new_refl = (upper_s[0] + times_f32(left_mid, upper_s[2])).astype(jnp.bfloat16)
    new_back = times_f32(left_sum, lower_s[1]).astype(jnp.bfloat16)
    new_fore = times_f32(right_sum, upper_s[2]).astype(jnp.bfloat16)
    new_under = (lower_s[3] + times_f32(right_mid, lower_s[1])).astype(jnp.bfloat16)
    return [new_refl, new_back, new_fore, new_under]


def assembled(pieces_ref, slot, own_piece):
    piece_count = pieces_ref.shape[0]
    return jnp.concatenate(
        [
            pieces_ref[(own_piece - source + piece_count) % piece_count, slot]
            for source in range(piece_count)
        ],
        axis=0,
    )


def star_rows(a11, a12, a21, a22, b11, b12, b21, b22):
    coupling_down = times_f32(b11, a22).astype(jnp.bfloat16)
    coupling_up = times_f32(a22, b11).astype(jnp.bfloat16)

    def round_trip(repeat, sums):
        left_sum, right_sum = sums
        left_sum = (a12 + times_f32(left_sum, coupling_down)).astype(jnp.bfloat16)
        right_sum = (b21 + times_f32(right_sum, coupling_up)).astype(jnp.bfloat16)
        return left_sum, right_sum

    left_sum, right_sum = lax.fori_loop(0, REFL, round_trip, (a12, b21))
    left_mid = times_f32(left_sum, b11).astype(jnp.bfloat16)
    right_mid = times_f32(right_sum, a22).astype(jnp.bfloat16)
    new_refl = (a11 + times_f32(left_mid, a21)).astype(jnp.bfloat16)
    new_back = times_f32(left_sum, b12).astype(jnp.bfloat16)
    new_fore = times_f32(right_sum, a21).astype(jnp.bfloat16)
    new_under = (b22 + times_f32(right_mid, b12)).astype(jnp.bfloat16)
    return new_refl, new_back, new_fore, new_under


def first_kernel(ctl_ref, modes_ref, scale_ref, top_ref, bottom_ref, whole_ref):
    own_piece = ctl_ref[0]
    row_count = top_ref.shape[1]
    for layer_pos in range(2):
        modes_one = modes_ref[layer_pos]
        modes_wide = modes_one.astype(jnp.float32)
        for kind in range(2):
            scaled = (modes_wide * scale_ref[layer_pos, kind]).astype(jnp.bfloat16)
            whole_ref[2 * layer_pos + kind] = lax.dot_general(
                modes_one,
                scaled,
                (((1,), (1,)), ((), ())),
                preferred_element_type=jnp.float32,
            ).astype(jnp.bfloat16)
    rows = pl.ds(pl.multiple_of(own_piece * row_count, row_count), row_count)
    new_refl, new_back, new_fore, new_under = star_rows(
        whole_ref[0, rows, :],
        whole_ref[1, rows, :],
        whole_ref[1],
        -whole_ref[0],
        whole_ref[2],
        whole_ref[3],
        whole_ref[3, rows, :],
        -whole_ref[2, rows, :],
    )
    top_ref[0] = new_under
    top_ref[1] = new_fore
    bottom_ref[0] = new_back
    bottom_ref[1] = new_refl


def level_kernel(ctl_ref, *refs):
    piece_count = len(refs) - 7
    far_refs, low_ref = refs[:piece_count], refs[piece_count]
    near_ref, top_ref, bottom_ref, new_top_ref, new_bottom_ref, whole_ref = refs[-6:]
    row_count = near_ref.shape[1]
    active = ctl_ref[0]
    own_piece = ctl_ref[1]

    @pl.when(active == 0)
    def _keep():
        new_top_ref[...] = top_ref[...]
        new_bottom_ref[...] = bottom_ref[...]

    @pl.when(active != 0)
    def _place():
        for shift in range(piece_count):
            source = (own_piece - shift + piece_count) % piece_count
            rows = pl.ds(pl.multiple_of(source * row_count, row_count), row_count)
            whole_ref[0:2, rows, :] = far_refs[shift][...]
        for source in range(piece_count):
            whole_ref[2:4, source * row_count : (source + 1) * row_count, :] = low_ref[source]

    @pl.when(active != 0)
    def _combine():
        a22 = whole_ref[0]
        a21 = whole_ref[1]
        b12 = whole_ref[2]
        b11 = whole_ref[3]
        a12 = near_ref[0]
        a11 = near_ref[1]
        b22 = top_ref[0]
        b21 = top_ref[1]
        new_refl, new_back, new_fore, new_under = star_rows(a11, a12, a21, a22, b11, b12, b21, b22)
        new_bottom_ref[1] = new_refl
        new_bottom_ref[0] = new_back
        new_top_ref[1] = new_fore
        new_top_ref[0] = new_under


def first_call(own_piece, row_count, modes_all, scales):
    ctl = own_piece.astype(jnp.int32).reshape(1)
    row_shape = jax.ShapeDtypeStruct((2, row_count, modes_all.shape[2]), modes_all.dtype)
    vmem = pl.BlockSpec(memory_space=pltpu.VMEM)
    whole_shape = (4, modes_all.shape[1], modes_all.shape[2])
    return pl.pallas_call(
        first_kernel,
        out_shape=(row_shape, row_shape),
        in_specs=[pl.BlockSpec(memory_space=pltpu.SMEM), vmem, vmem],
        out_specs=(vmem, vmem),
        scratch_shapes=[pltpu.VMEM(whole_shape, modes_all.dtype)],
    )(ctl, modes_all, scales)


def level_call(active, own_piece, far, low, near, top, bottom):
    ctl = jnp.stack([active.astype(jnp.int32), own_piece.astype(jnp.int32)])
    row_shape = jax.ShapeDtypeStruct(top.shape, top.dtype)
    whole_shape = (4, far[0].shape[1] * len(far), far[0].shape[2])
    vmem = pl.BlockSpec(memory_space=pltpu.VMEM)
    return pl.pallas_call(
        level_kernel,
        out_shape=(row_shape, row_shape),
        in_specs=[pl.BlockSpec(memory_space=pltpu.SMEM)] + [vmem] * (len(far) + 4),
        out_specs=(vmem, vmem),
        scratch_shapes=[pltpu.VMEM(whole_shape, top.dtype)],
    )(ctl, *far, low, near, top, bottom)


def spread(value, axis):
    count = lax.axis_size(axis)
    return [value] + [rotated(value, axis, shift) for shift in range(1, count)]


def on_device(mode_matrix, decay_rate, facet_refl):
    coefficients = jnp.stack([decay_rate, facet_refl], axis=-1)
    relayed_modes = lax.all_to_all(mode_matrix, "layer", split_axis=0, concat_axis=1, tiled=True)
    relayed_coeff = lax.all_to_all(coefficients, "layer", split_axis=0, concat_axis=1, tiled=True)
    relayed_decay = relayed_coeff[..., 0]
    relayed_refl = relayed_coeff[..., 1]
    block_index = lax.axis_index("blk")
    block_count = lax.axis_size("blk")
    refl_full = relayed_refl.astype(jnp.float32)
    transmit = jnp.sqrt(1.0 - refl_full * refl_full) * jnp.exp(-relayed_decay.astype(jnp.float32))
    modes_all = lax.all_gather(relayed_modes, "blk", axis=2, tiled=True)
    scales = jnp.stack([refl_full, transmit], axis=1)[:, :, None, :]
    row_count = HARM // block_count
    own_top, own_bottom = first_call(block_index, row_count, modes_all, scales)
    group_index = lax.axis_index("layer")
    level_count = lax.axis_size("layer").bit_length() - 1
    for section_level in range(level_count):
        distance = 1 << section_level
        lower_far = lax.all_gather(own_bottom, "blk", axis=0, tiled=False)
        upper_top = passed_along(own_top, "layer", distance)
        upper_bottom = passed_along(own_bottom, "layer", distance)
        upper_far = spread(upper_top, "blk")
        own_top, own_bottom = level_call(
            group_index >= distance,
            block_index,
            upper_far,
            lower_far,
            upper_bottom,
            own_top,
            own_bottom,
        )
    own_rows = jnp.stack([own_bottom[1], own_bottom[0], own_top[1], own_top[0]])
    return own_rows[None]


def solution(mesh):
    placed = (P(None, "layer", "blk"), P(None, "layer"), P(None, "layer"))
    return jax.shard_map(
        on_device,
        mesh=mesh,
        in_specs=placed,
        out_specs=P("layer", None, "blk", None),
        check_vma=False,
    )
```

```python
import functools

import jax
import jax.numpy as jnp
from jax import lax
from jax.sharding import PartitionSpec as P
from jax.experimental import pallas as pl
from jax.experimental.pallas import tpu as pltpu

HARM = 512
REFL = 4


def passed_along(value, axis, steps):
    count = lax.axis_size(axis)
    first, last = (max(0, -steps), min(count, count - steps))
    return lax.ppermute(value, axis, [(source, source + steps) for source in range(first, last)])


def rotated(value, axis, steps):
    count = lax.axis_size(axis)
    return lax.ppermute(value, axis, [(source, (source + steps) % count) for source in range(count)])


def times_f32(left_op, right_op):
    return jnp.dot(left_op, right_op, preferred_element_type=jnp.float32)


def star_whole(upper_s, lower_s):
    coupling_down = times_f32(lower_s[0], upper_s[3]).astype(jnp.bfloat16)
    coupling_up = times_f32(upper_s[3], lower_s[0]).astype(jnp.bfloat16)
    left_sum = upper_s[1]
    for repeat in range(REFL):
        left_sum = (upper_s[1] + times_f32(left_sum, coupling_down)).astype(jnp.bfloat16)
    right_sum = lower_s[2]
    for repeat in range(REFL):
        right_sum = (lower_s[2] + times_f32(right_sum, coupling_up)).astype(jnp.bfloat16)
    left_mid = times_f32(left_sum, lower_s[0]).astype(jnp.bfloat16)
    right_mid = times_f32(right_sum, upper_s[3]).astype(jnp.bfloat16)
    new_refl = (upper_s[0] + times_f32(left_mid, upper_s[2])).astype(jnp.bfloat16)
    new_back = times_f32(left_sum, lower_s[1]).astype(jnp.bfloat16)
    new_fore = times_f32(right_sum, upper_s[2]).astype(jnp.bfloat16)
    new_under = (lower_s[3] + times_f32(right_mid, lower_s[1])).astype(jnp.bfloat16)
    return [new_refl, new_back, new_fore, new_under]


def assembled(pieces_ref, slot, own_piece):
    piece_count = pieces_ref.shape[0]
    return jnp.concatenate(
        [
            pieces_ref[(own_piece - source + piece_count) % piece_count, slot]
            for source in range(piece_count)
        ],
        axis=0,
    )


def star_rows(a11, a12, a21, a22, b11, b12, b21, b22):
    coupling_down = times_f32(b11, a22).astype(jnp.bfloat16)
    coupling_up = times_f32(a22, b11).astype(jnp.bfloat16)
    left_sum = a12
    for repeat in range(REFL):
        left_sum = (a12 + times_f32(left_sum, coupling_down)).astype(jnp.bfloat16)
    right_sum = b21
    for repeat in range(REFL):
        right_sum = (b21 + times_f32(right_sum, coupling_up)).astype(jnp.bfloat16)
    left_mid = times_f32(left_sum, b11).astype(jnp.bfloat16)
    right_mid = times_f32(right_sum, a22).astype(jnp.bfloat16)
    new_refl = (a11 + times_f32(left_mid, a21)).astype(jnp.bfloat16)
    new_back = times_f32(left_sum, b12).astype(jnp.bfloat16)
    new_fore = times_f32(right_sum, a21).astype(jnp.bfloat16)
    new_under = (b22 + times_f32(right_mid, b12)).astype(jnp.bfloat16)
    return new_refl, new_back, new_fore, new_under


def first_kernel(ctl_ref, modes_ref, scale_ref, top_ref, bottom_ref, *refs):
    low_refs, (whole_ref, new_ref) = refs[:-2], refs[-2:]
    piece_count = len(low_refs)
    own_piece = ctl_ref[0]
    row_count = top_ref.shape[1]
    for layer_pos in range(2):
        modes_one = modes_ref[layer_pos]
        modes_wide = modes_one.astype(jnp.float32)
        for kind in range(2):
            scaled = (modes_wide * scale_ref[layer_pos, kind]).astype(jnp.bfloat16)
            whole_ref[2 * layer_pos + kind] = lax.dot_general(
                modes_one,
                scaled,
                (((1,), (1,)), ((), ())),
                preferred_element_type=jnp.float32,
            ).astype(jnp.bfloat16)
    new_refl, new_back, new_fore, new_under = star_rows(
        whole_ref[0],
        whole_ref[1],
        whole_ref[1],
        -whole_ref[0],
        whole_ref[2],
        whole_ref[3],
        whole_ref[3],
        -whole_ref[2],
    )
    new_ref[0] = new_under
    new_ref[1] = new_fore
    new_ref[2] = new_back
    new_ref[3] = new_refl
    rows = pl.ds(pl.multiple_of(own_piece * row_count, row_count), row_count)
    top_ref[...] = new_ref[0:2, rows, :]
    bottom_ref[...] = new_ref[2:4, rows, :]
    for shift, low_ref in enumerate(low_refs):
        source = (own_piece - shift + piece_count) % piece_count
        low_ref[...] = new_ref[2:4, pl.ds(pl.multiple_of(source * row_count, row_count), row_count), :]


def level_kernel(ctl_ref, *refs):
    piece_count = (len(refs) - 6) // 2
    far_refs, low_refs = refs[:piece_count], refs[piece_count : 2 * piece_count]
    near_ref, top_ref, bottom_ref, new_top_ref, new_bottom_ref, whole_ref = refs[-6:]
    row_count = near_ref.shape[1]
    active = ctl_ref[0]
    own_piece = ctl_ref[1]

    @pl.when(active == 0)
    def _keep():
        new_top_ref[...] = top_ref[...]
        new_bottom_ref[...] = bottom_ref[...]

    @pl.when(active != 0)
    def _place():
        for shift in range(piece_count):
            source = (own_piece - shift + piece_count) % piece_count
            rows = pl.ds(pl.multiple_of(source * row_count, row_count), row_count)
            whole_ref[0:2, rows, :] = far_refs[shift][...]
            whole_ref[2:4, rows, :] = low_refs[shift][...]

    @pl.when(active != 0)
    def _combine():
        a22 = whole_ref[0]
        a21 = whole_ref[1]
        b12 = whole_ref[2]
        b11 = whole_ref[3]
        a12 = near_ref[0]
        a11 = near_ref[1]
        b22 = top_ref[0]
        b21 = top_ref[1]
        new_refl, new_back, new_fore, new_under = star_rows(a11, a12, a21, a22, b11, b12, b21, b22)
        new_bottom_ref[1] = new_refl
        new_bottom_ref[0] = new_back
        new_top_ref[1] = new_fore
        new_top_ref[0] = new_under


def first_call(own_piece, row_count, piece_count, modes_all, scales):
    ctl = own_piece.astype(jnp.int32).reshape(1)
    row_shape = jax.ShapeDtypeStruct((2, row_count, modes_all.shape[2]), modes_all.dtype)
    vmem = pl.BlockSpec(memory_space=pltpu.VMEM)
    whole_shape = (4, modes_all.shape[1], modes_all.shape[2])
    return pl.pallas_call(
        first_kernel,
        out_shape=(row_shape,) * (2 + piece_count),
        in_specs=[pl.BlockSpec(memory_space=pltpu.SMEM), vmem, vmem],
        out_specs=(vmem,) * (2 + piece_count),
        scratch_shapes=[pltpu.VMEM(whole_shape, modes_all.dtype)] * 2,
    )(ctl, modes_all, scales)


def level_call(active, own_piece, far, low, near, top, bottom):
    ctl = jnp.stack([active.astype(jnp.int32), own_piece.astype(jnp.int32)])
    row_shape = jax.ShapeDtypeStruct(top.shape, top.dtype)
    whole_shape = (4, far[0].shape[1] * len(far), far[0].shape[2])
    vmem = pl.BlockSpec(memory_space=pltpu.VMEM)
    return pl.pallas_call(
        level_kernel,
        out_shape=(row_shape, row_shape),
        in_specs=[pl.BlockSpec(memory_space=pltpu.SMEM)] + [vmem] * (2 * len(far) + 3),
        out_specs=(vmem, vmem),
        scratch_shapes=[pltpu.VMEM(whole_shape, top.dtype)],
    )(ctl, *far, *low, near, top, bottom)


def spread(value, axis):
    count = lax.axis_size(axis)
    return [value] + [rotated(value, axis, shift) for shift in range(1, count)]


def on_device(mode_matrix, decay_rate, facet_refl):
    coefficients = jnp.stack([decay_rate, facet_refl], axis=-1)
    relayed_modes = lax.all_to_all(mode_matrix, "layer", split_axis=0, concat_axis=1, tiled=True)
    relayed_coeff = lax.all_to_all(coefficients, "layer", split_axis=0, concat_axis=1, tiled=True)
    relayed_decay = relayed_coeff[..., 0]
    relayed_refl = relayed_coeff[..., 1]
    block_index = lax.axis_index("blk")
    block_count = lax.axis_size("blk")
    refl_full = relayed_refl.astype(jnp.float32)
    transmit = jnp.sqrt(1.0 - refl_full * refl_full) * jnp.exp(-relayed_decay.astype(jnp.float32))
    modes_all = lax.all_gather(relayed_modes, "blk", axis=2, tiled=True)
    scales = jnp.stack([refl_full, transmit], axis=1)[:, :, None, :]
    row_count = HARM // block_count
    own_top, own_bottom, *first_low = first_call(
        block_index, row_count, block_count, modes_all, scales
    )
    group_index = lax.axis_index("layer")
    level_count = lax.axis_size("layer").bit_length() - 1
    for section_level in range(level_count):
        distance = 1 << section_level
        lower_far = first_low if section_level == 0 else spread(own_bottom, "blk")
        upper_top = passed_along(own_top, "layer", distance)
        upper_bottom = passed_along(own_bottom, "layer", distance)
        upper_far = spread(upper_top, "blk")
        own_top, own_bottom = level_call(
            group_index >= distance,
            block_index,
            upper_far,
            lower_far,
            upper_bottom,
            own_top,
            own_bottom,
        )
    own_rows = jnp.stack([own_bottom[1], own_bottom[0], own_top[1], own_top[0]])
    return own_rows[None]


def solution(mesh):
    placed = (P(None, "layer", "blk"), P(None, "layer"), P(None, "layer"))
    return jax.shard_map(
        on_device,
        mesh=mesh,
        in_specs=placed,
        out_specs=P("layer", None, "blk", None),
        check_vma=False,
    )
```

```python
import functools

import jax
import jax.numpy as jnp
from jax import lax
from jax.sharding import PartitionSpec as P
from jax.experimental import pallas as pl
from jax.experimental.pallas import tpu as pltpu

HARM = 512
REFL = 4


def passed_along(value, axis, steps):
    count = lax.axis_size(axis)
    first, last = (max(0, -steps), min(count, count - steps))
    return lax.ppermute(value, axis, [(source, source + steps) for source in range(first, last)])


def rotated(value, axis, steps):
    count = lax.axis_size(axis)
    return lax.ppermute(value, axis, [(source, (source + steps) % count) for source in range(count)])


def times_f32(left_op, right_op):
    return jnp.dot(left_op, right_op, preferred_element_type=jnp.float32)


def star_whole(upper_s, lower_s):
    coupling_down = times_f32(lower_s[0], upper_s[3]).astype(jnp.bfloat16)
    coupling_up = times_f32(upper_s[3], lower_s[0]).astype(jnp.bfloat16)
    left_sum = upper_s[1]
    for repeat in range(REFL):
        left_sum = (upper_s[1] + times_f32(left_sum, coupling_down)).astype(jnp.bfloat16)
    right_sum = lower_s[2]
    for repeat in range(REFL):
        right_sum = (lower_s[2] + times_f32(right_sum, coupling_up)).astype(jnp.bfloat16)
    left_mid = times_f32(left_sum, lower_s[0]).astype(jnp.bfloat16)
    right_mid = times_f32(right_sum, upper_s[3]).astype(jnp.bfloat16)
    new_refl = (upper_s[0] + times_f32(left_mid, upper_s[2])).astype(jnp.bfloat16)
    new_back = times_f32(left_sum, lower_s[1]).astype(jnp.bfloat16)
    new_fore = times_f32(right_sum, upper_s[2]).astype(jnp.bfloat16)
    new_under = (lower_s[3] + times_f32(right_mid, lower_s[1])).astype(jnp.bfloat16)
    return [new_refl, new_back, new_fore, new_under]


def assembled(pieces_ref, slot, own_piece):
    piece_count = pieces_ref.shape[0]
    return jnp.concatenate(
        [
            pieces_ref[(own_piece - source + piece_count) % piece_count, slot]
            for source in range(piece_count)
        ],
        axis=0,
    )


def star_rows(a11, a12, a21, a22, b11, b12, b21, b22):
    coupling_down = times_f32(b11, a22).astype(jnp.bfloat16)
    coupling_up = times_f32(a22, b11).astype(jnp.bfloat16)
    left_sum = a12
    for repeat in range(REFL):
        left_sum = (a12 + times_f32(left_sum, coupling_down)).astype(jnp.bfloat16)
    right_sum = b21
    for repeat in range(REFL):
        right_sum = (b21 + times_f32(right_sum, coupling_up)).astype(jnp.bfloat16)
    left_mid = times_f32(left_sum, b11).astype(jnp.bfloat16)
    right_mid = times_f32(right_sum, a22).astype(jnp.bfloat16)
    new_refl = (a11 + times_f32(left_mid, a21)).astype(jnp.bfloat16)
    new_back = times_f32(left_sum, b12).astype(jnp.bfloat16)
    new_fore = times_f32(right_sum, a21).astype(jnp.bfloat16)
    new_under = (b22 + times_f32(right_mid, b12)).astype(jnp.bfloat16)
    return new_refl, new_back, new_fore, new_under


def first_kernel(ctl_ref, modes_ref, scale_ref, top_ref, bottom_ref, *refs):
    piece_count = (len(refs) - 2) // 2
    low_refs, far_refs = refs[:piece_count], refs[piece_count : 2 * piece_count]
    whole_ref, new_ref = refs[-2:]
    own_piece = ctl_ref[0]
    row_count = top_ref.shape[1]
    for layer_pos in range(2):
        modes_one = modes_ref[layer_pos]
        modes_wide = modes_one.astype(jnp.float32)
        for kind in range(2):
            scaled = (modes_wide * scale_ref[layer_pos, kind]).astype(jnp.bfloat16)
            whole_ref[2 * layer_pos + kind] = lax.dot_general(
                modes_one,
                scaled,
                (((1,), (1,)), ((), ())),
                preferred_element_type=jnp.float32,
            ).astype(jnp.bfloat16)
    new_refl, new_back, new_fore, new_under = star_rows(
        whole_ref[0],
        whole_ref[1],
        whole_ref[1],
        -whole_ref[0],
        whole_ref[2],
        whole_ref[3],
        whole_ref[3],
        -whole_ref[2],
    )
    new_ref[0] = new_under
    new_ref[1] = new_fore
    new_ref[2] = new_back
    new_ref[3] = new_refl
    rows = pl.ds(pl.multiple_of(own_piece * row_count, row_count), row_count)
    top_ref[...] = new_ref[0:2, rows, :]
    bottom_ref[...] = new_ref[2:4, rows, :]
    for shift, low_ref in enumerate(low_refs):
        source = (own_piece - shift + piece_count) % piece_count
        low_ref[...] = new_ref[2:4, pl.ds(pl.multiple_of(source * row_count, row_count), row_count), :]
        far_refs[shift][...] = new_ref[
            0:2, pl.ds(pl.multiple_of(source * row_count, row_count), row_count), :
        ]


def level_kernel(ctl_ref, *refs):
    piece_count = (len(refs) - 6) // 2
    far_refs, low_refs = refs[:piece_count], refs[piece_count : 2 * piece_count]
    near_ref, top_ref, bottom_ref, new_top_ref, new_bottom_ref, whole_ref = refs[-6:]
    row_count = near_ref.shape[1]
    active = ctl_ref[0]
    own_piece = ctl_ref[1]

    @pl.when(active == 0)
    def _keep():
        new_top_ref[...] = top_ref[...]
        new_bottom_ref[...] = bottom_ref[...]

    @pl.when(active != 0)
    def _place():
        for shift in range(piece_count):
            source = (own_piece - shift + piece_count) % piece_count
            rows = pl.ds(pl.multiple_of(source * row_count, row_count), row_count)
            whole_ref[0:2, rows, :] = far_refs[shift][...]
            whole_ref[2:4, rows, :] = low_refs[shift][...]

    @pl.when(active != 0)
    def _combine():
        a22 = whole_ref[0]
        a21 = whole_ref[1]
        b12 = whole_ref[2]
        b11 = whole_ref[3]
        a12 = near_ref[0]
        a11 = near_ref[1]
        b22 = top_ref[0]
        b21 = top_ref[1]
        new_refl, new_back, new_fore, new_under = star_rows(a11, a12, a21, a22, b11, b12, b21, b22)
        new_bottom_ref[1] = new_refl
        new_bottom_ref[0] = new_back
        new_top_ref[1] = new_fore
        new_top_ref[0] = new_under


def first_call(own_piece, row_count, piece_count, modes_all, scales):
    ctl = own_piece.astype(jnp.int32).reshape(1)
    row_shape = jax.ShapeDtypeStruct((2, row_count, modes_all.shape[2]), modes_all.dtype)
    vmem = pl.BlockSpec(memory_space=pltpu.VMEM)
    whole_shape = (4, modes_all.shape[1], modes_all.shape[2])
    return pl.pallas_call(
        first_kernel,
        out_shape=(row_shape,) * (2 + 2 * piece_count),
        in_specs=[pl.BlockSpec(memory_space=pltpu.SMEM), vmem, vmem],
        out_specs=(vmem,) * (2 + 2 * piece_count),
        scratch_shapes=[pltpu.VMEM(whole_shape, modes_all.dtype)] * 2,
    )(ctl, modes_all, scales)


def level_call(active, own_piece, far, low, near, top, bottom):
    ctl = jnp.stack([active.astype(jnp.int32), own_piece.astype(jnp.int32)])
    row_shape = jax.ShapeDtypeStruct(top.shape, top.dtype)
    whole_shape = (4, far[0].shape[1] * len(far), far[0].shape[2])
    vmem = pl.BlockSpec(memory_space=pltpu.VMEM)
    return pl.pallas_call(
        level_kernel,
        out_shape=(row_shape, row_shape),
        in_specs=[pl.BlockSpec(memory_space=pltpu.SMEM)] + [vmem] * (2 * len(far) + 3),
        out_specs=(vmem, vmem),
        scratch_shapes=[pltpu.VMEM(whole_shape, top.dtype)],
    )(ctl, *far, *low, near, top, bottom)


def spread(value, axis):
    count = lax.axis_size(axis)
    return [value] + [rotated(value, axis, shift) for shift in range(1, count)]


def on_device(mode_matrix, decay_rate, facet_refl):
    coefficients = jnp.stack([decay_rate, facet_refl], axis=-1)
    relayed_modes = lax.all_to_all(mode_matrix, "layer", split_axis=0, concat_axis=1, tiled=True)
    relayed_coeff = lax.all_to_all(coefficients, "layer", split_axis=0, concat_axis=1, tiled=True)
    relayed_decay = relayed_coeff[..., 0]
    relayed_refl = relayed_coeff[..., 1]
    block_index = lax.axis_index("blk")
    block_count = lax.axis_size("blk")
    refl_full = relayed_refl.astype(jnp.float32)
    transmit = jnp.sqrt(1.0 - refl_full * refl_full) * jnp.exp(-relayed_decay.astype(jnp.float32))
    modes_all = lax.all_gather(relayed_modes, "blk", axis=2, tiled=True)
    scales = jnp.stack([refl_full, transmit], axis=1)[:, :, None, :]
    row_count = HARM // block_count
    own_top, own_bottom, *first_pieces = first_call(
        block_index, row_count, block_count, modes_all, scales
    )
    first_low, first_far = first_pieces[:block_count], first_pieces[block_count:]
    group_index = lax.axis_index("layer")
    level_count = lax.axis_size("layer").bit_length() - 1
    for section_level in range(level_count):
        distance = 1 << section_level
        lower_far = first_low if section_level == 0 else spread(own_bottom, "blk")
        upper_bottom = passed_along(own_bottom, "layer", distance)
        if section_level == 0:
            upper_far = [passed_along(piece, "layer", distance) for piece in first_far]
        else:
            upper_far = spread(passed_along(own_top, "layer", distance), "blk")
        own_top, own_bottom = level_call(
            group_index >= distance,
            block_index,
            upper_far,
            lower_far,
            upper_bottom,
            own_top,
            own_bottom,
        )
    own_rows = jnp.stack([own_bottom[1], own_bottom[0], own_top[1], own_top[0]])
    return own_rows[None]


def solution(mesh):
    placed = (P(None, "layer", "blk"), P(None, "layer"), P(None, "layer"))
    return jax.shard_map(
        on_device,
        mesh=mesh,
        in_specs=placed,
        out_specs=P("layer", None, "blk", None),
        check_vma=False,
    )
```
